256 devices in a mesh: dm: 32 (over x_lo, z, core), beam: 8 (over y, x_hi).
Axes of the slice: x: 4 (x_hi: 2, x_lo: 2; x = x_hi * 2 + x_lo), y: 4, z: 8, core: 2. Of those that a mesh axis runs over, the one named last changes fastest.
Arguments:
- voltages: bfloat16 [4096, 8, 2, 256], P(('beam', 'dm')), may hold values from -6 to 6
- responses: bfloat16 [128, 4096, 2, 256], P('dm', 'beam'), may hold values from -6 to 6
- chirp_len: int32 [128], P('dm'), may hold values from 1 to 128, as said below
Outputs:
- detected: bfloat16 [128, 8, 262144], P('dm', 'beam')
The draws below stay inside these ranges and needn't reach their ends.
Inputs may be any that keep to these rules, and one draw needn't show every extreme that they name: `chirp_len`: some trial has the longest chirp 256 // 2 and some trial a chirp of 1 sample.
All inputs are finite; a program needn't handle non-finite values.
Results may differ from the reference program's by a relative error of at most 0.0054.
Values may be sent and summed in bfloat16 or wider, within the bound.
No kernel may reach another device: no remote copies, remote signals or barrier semaphores. Data moves between devices by JAX's collectives and lax.ppermute only.
A program may use at most 128 MiB of HBM per device.

```python
import math
import jax
import jax.numpy as jnp
from jax import lax

CH = 4096
L = 256
RATE = 4
DMS = 128
BEAMS = 8
TOUT = 64


def draw_chirp_len(key, part):
    values = jax.random.randint(key, (DMS,), 1, L // 2 + 1, dtype=jnp.int32)
    chosen = jax.random.randint(jax.random.fold_in(key, 7), (), 0, DMS, dtype=jnp.int32)
    values = values.at[chosen].set(L // 2)
    values = values.at[(chosen + 1) % DMS].set(1)
    return values


def block_levels(own_key, shape, pieces, smallest, top_value):
    def one(dim, parts):
        heights = jax.random.uniform(jax.random.fold_in(jax.random.fold_in(own_key, 6), dim), (parts,), jnp.float32, smallest / len(pieces), top_value / len(pieces))
        return jnp.repeat(jnp.exp(heights), shape[dim] // parts).reshape((-1,) + (1,) * (len(shape) - dim - 1))

    loudness = one(*pieces[0])
    for cut in pieces[1:]:
        loudness = loudness * one(*cut)
    return loudness


def bell_draw(rng, shape, width, limit, pieces=(), held_as=jnp.bfloat16):
    array = width * jax.random.normal(rng, shape, jnp.float32)
    if pieces:
        array = array * block_levels(rng, shape, pieces, -0.22, 0.18)
    return jnp.clip(array, -limit, limit).astype(held_as)


def setup_inputs(seed: int = 0) -> dict:
    arg_keys = jax.random.split(jax.random.key(seed), 4)
    return {
        "voltages": bell_draw(arg_keys[0], (CH, BEAMS, 2, L), 0.7, 6.0, ((0, 256),)),
        "responses": bell_draw(arg_keys[1], (DMS, CH, 2, L), 0.7, 6.0, ((0, 32), (1, 8))),
        "chirp_len": draw_chirp_len(jax.random.fold_in(arg_keys[3], 71), 0),
    }


def dft_tables(length):
    sample = jnp.arange(length, dtype=jnp.int32)
    phases = sample[:, None] * sample[None, :] % length
    angles = phases.astype(jnp.float32) * (2.0 * math.pi / length)
    cosine = jnp.cos(angles) / math.sqrt(length)
    sine_part = jnp.sin(angles) / math.sqrt(length)
    forward = jnp.concatenate([jnp.concatenate([cosine, -sine_part], 1), jnp.concatenate([sine_part, cosine], 1)], 0)
    backward = jnp.concatenate([jnp.concatenate([cosine, sine_part], 1), jnp.concatenate([-sine_part, cosine], 1)], 0)
    return (forward.astype(jnp.bfloat16), backward.astype(jnp.bfloat16))

def spectrum(signal, forward):
    length = signal.shape[-1]
    flattened = signal.reshape(-1, 2 * length)
    result = jnp.dot(flattened, forward, preferred_element_type=jnp.float32)
    return result.astype(jnp.bfloat16).reshape(signal.shape)

def detect(spectra, response, lengths, backward, rate):
    chans = spectra.shape[0]
    beam_count = spectra.shape[1]
    length = spectra.shape[-1]
    samples_out = length // rate
    spec_re = spectra[:, :, 0, :].astype(jnp.float32)
    spec_im = spectra[:, :, 1, :].astype(jnp.float32)
    sample = jnp.arange(length, dtype=jnp.int32)

    def one_trial(trial):
        filter_row, chirp = trial
        resp_re = filter_row[:, 0, :].astype(jnp.float32)[:, None, :]
        resp_im = filter_row[:, 1, :].astype(jnp.float32)[:, None, :]
        real_part = resp_re * spec_re - resp_im * spec_im
        imag_part = resp_re * spec_im + resp_im * spec_re
        joined = jnp.concatenate([real_part, imag_part], -1).astype(jnp.bfloat16)
        series = jnp.dot(joined.reshape(-1, 2 * length), backward, preferred_element_type=jnp.float32)
        series = series.reshape(chans, beam_count, 2 * length)
        powers = series[..., :length] ** 2 + series[..., length:] ** 2
        valid_mask = sample >= chirp
        powers = jnp.where(valid_mask[None, None, :], powers, jnp.float32(0.0))
        binned = powers.reshape(chans, beam_count, samples_out, rate).sum(-1) / rate
        return jnp.transpose(binned, (1, 0, 2)).astype(jnp.bfloat16)
    return lax.map(one_trial, (response, lengths))

def reference(voltages, responses, chirp_len):
    forward, backward = dft_tables(L)
    spectra = spectrum(voltages, forward)
    result = detect(spectra, responses, chirp_len, backward, RATE)
    return result.reshape(DMS, BEAMS, CH * TOUT)
```

```python
import functools
import math

import jax
import jax.numpy as jnp
from jax import lax
from jax.experimental import pallas as pl
from jax.experimental.pallas import tpu as pltpu
from jax.sharding import PartitionSpec as P

RATE = 4
CHAN_BLOCK = 256


def dft_tables(length):
    sample = jnp.arange(length, dtype=jnp.int32)
    phases = sample[:, None] * sample[None, :] % length
    angles = phases.astype(jnp.float32) * (2.0 * math.pi / length)
    cosine = jnp.cos(angles) / math.sqrt(length)
    sine_part = jnp.sin(angles) / math.sqrt(length)
    forward = jnp.concatenate(
        [jnp.concatenate([cosine, -sine_part], 1), jnp.concatenate([sine_part, cosine], 1)], 0
    )
    backward = jnp.concatenate(
        [jnp.concatenate([cosine, sine_part], 1), jnp.concatenate([-sine_part, cosine], 1)], 0
    )
    return (forward.astype(jnp.bfloat16), backward.astype(jnp.bfloat16))


def sample_order(length, rate):
    pos = jnp.arange(length, dtype=jnp.int32)
    bins = length // rate
    return rate * (pos % bins) + pos // bins


def detect_kernel(chirp_ref, spec_ref, resp_ref, back_ref, out_ref, pair_ref):
    d = pl.program_id(1)
    beams, chans, width = spec_ref.shape
    length = width // 2
    bins = length // RATE
    x = spec_ref[...]
    xr = x[:, :, :length].astype(jnp.float32)
    xi = x[:, :, length:].astype(jnp.float32)
    h = resp_ref[0]
    hr = h[:, :length].astype(jnp.float32)[None]
    hi = h[:, length:].astype(jnp.float32)[None]
    fr = hr * xr - hi * xi
    fi = hr * xi + hi * xr
    joined = jnp.concatenate([fr, fi], -1).reshape(beams * chans, width).astype(jnp.bfloat16)
    series = jnp.dot(joined, back_ref[...], preferred_element_type=jnp.float32)
    powers = series[:, :length] ** 2 + series[:, length:] ** 2
    pos = lax.broadcasted_iota(jnp.int32, (1, length), 1)
    t = RATE * (pos % bins) + pos // bins
    powers = jnp.where(t >= chirp_ref[d], powers, jnp.float32(0.0))
    half = powers[:, : length // 2] + powers[:, length // 2 :]
    pair_ref[...] = half + pltpu.roll(half, bins, 1)
    rows = beams * chans // 2
    even = pair_ref[pl.ds(0, rows, stride=2), :]
    odd = pair_ref[pl.ds(1, rows, stride=2), :]
    lane = lax.broadcasted_iota(jnp.int32, (1, 2 * bins), 1)
    both = jnp.where(lane < bins, even, odd) / RATE
    out_ref[0] = both.reshape(beams, chans // 2, 2 * bins).astype(out_ref.dtype)


def detect(spectra, responses, chirp_len, backward):
    beams, chans, width = spectra.shape
    trials = responses.shape[0]
    length = width // 2
    bins = length // RATE
    block = min(CHAN_BLOCK, chans)
    grid = (chans // block, trials)
    flops = 2 * trials * beams * chans * width * width
    bytes_accessed = 2 * (spectra.size + responses.size + backward.size + trials * beams * chans * bins)
    return pl.pallas_call(
        detect_kernel,
        out_shape=jax.ShapeDtypeStruct((trials, beams, chans // 2, 2 * bins), jnp.bfloat16),
        grid_spec=pltpu.PrefetchScalarGridSpec(
            num_scalar_prefetch=1,
            grid=grid,
            in_specs=[
                pl.BlockSpec((beams, block, width), lambda c, d, cl: (0, c, 0)),
                pl.BlockSpec((1, block, width), lambda c, d, cl: (d, c, 0)),
                pl.BlockSpec((width, width), lambda c, d, cl: (0, 0)),
            ],
            out_specs=pl.BlockSpec((1, beams, block // 2, 2 * bins), lambda c, d, cl: (d, 0, c, 0)),
            scratch_shapes=[pltpu.VMEM((beams * block, 2 * bins), jnp.float32)],
        ),
        compiler_params=pltpu.CompilerParams(
            dimension_semantics=("arbitrary", "arbitrary"), vmem_limit_bytes=48 * 1024 * 1024
        ),
        cost_estimate=pl.CostEstimate(flops=flops, transcendentals=0, bytes_accessed=bytes_accessed),
    )(chirp_len, spectra, responses, backward)


def shards(voltages, responses, chirp_len):
    chans_local, beams, _, length = voltages.shape
    trials, chans = responses.shape[0], responses.shape[1]
    forward, backward = dft_tables(length)
    order = sample_order(length, RATE)
    backward = jnp.concatenate([backward[:, order], backward[:, length + order]], 1)
    local = jnp.dot(
        voltages.reshape(-1, 2 * length), forward, preferred_element_type=jnp.float32
    ).astype(jnp.bfloat16)
    local = local.reshape(chans_local, beams, 2 * length).transpose(1, 0, 2)
    spectra = lax.all_gather(local, "dm", axis=1, tiled=True)
    detected = detect(spectra, responses.reshape(trials, chans, 2 * length), chirp_len, backward)
    flattened = detected.reshape(trials, beams, -1)
    return lax.all_to_all(flattened, "beam", split_axis=1, concat_axis=2, tiled=True)


def solution(mesh):
    placed = (P(("beam", "dm"), None, None, None), P("dm", "beam", None, None), P("dm"))
    return jax.shard_map(
        shards, mesh=mesh, in_specs=placed, out_specs=P("dm", "beam", None), check_vma=False
    )
```

```python
import functools
import math

import jax
import jax.numpy as jnp
from jax import lax
from jax.experimental import pallas as pl
from jax.experimental.pallas import tpu as pltpu
from jax.sharding import PartitionSpec as P

RATE = 4
CHAN_BLOCK = 256


def dft_tables(length):
    sample = jnp.arange(length, dtype=jnp.int32)
    phases = sample[:, None] * sample[None, :] % length
    angles = phases.astype(jnp.float32) * (2.0 * math.pi / length)
    cosine = jnp.cos(angles) / math.sqrt(length)
    sine_part = jnp.sin(angles) / math.sqrt(length)
    forward = jnp.concatenate(
        [jnp.concatenate([cosine, -sine_part], 1), jnp.concatenate([sine_part, cosine], 1)], 0
    )
    backward = jnp.concatenate(
        [jnp.concatenate([cosine, sine_part], 1), jnp.concatenate([-sine_part, cosine], 1)], 0
    )
    return (forward.astype(jnp.bfloat16), backward.astype(jnp.bfloat16))


def sample_order(length, rate):
    pos = jnp.arange(length, dtype=jnp.int32)
    bins = length // rate
    return rate * (pos % bins) + pos // bins


def detect_kernel(chirp_ref, spec_ref, resp_ref, back_ref, out_ref, pair_ref):
    d = pl.program_id(1)
    beams, chans, width = spec_ref.shape
    length = width // 2
    bins = length // RATE
    x = spec_ref[...]
    xr = x[:, :, :length].astype(jnp.float32)
    xi = x[:, :, length:].astype(jnp.float32)
    h = resp_ref[0]
    hr = h[:, :length].astype(jnp.float32)[None]
    hi = h[:, length:].astype(jnp.float32)[None]
    fr = hr * xr - hi * xi
    fi = hr * xi + hi * xr
    joined = jnp.concatenate([fr, fi], -1).reshape(beams * chans, width).astype(jnp.bfloat16)
    series = jnp.dot(joined, back_ref[...], preferred_element_type=jnp.float32)
    powers = series[:, :length] ** 2 + series[:, length:] ** 2
    pos = lax.broadcasted_iota(jnp.int32, (1, length), 1)
    t = RATE * (pos % bins) + pos // bins
    powers = jnp.where(t >= chirp_ref[d], powers, jnp.float32(0.0))
    half = powers[:, : length // 2] + powers[:, length // 2 :]
    pair_ref[...] = half + pltpu.roll(half, bins, 1)
    rows = beams * chans // 2
    even = pair_ref[pl.ds(0, rows, stride=2), :]
    odd = pair_ref[pl.ds(1, rows, stride=2), :]
    lane = lax.broadcasted_iota(jnp.int32, (1, 2 * bins), 1)
    both = jnp.where(lane < bins, even, odd) / RATE
    out_ref[0] = both.reshape(beams, chans // 2, 2 * bins).astype(out_ref.dtype)


def detect(spectra, responses, chirp_len, backward):
    beams, chans, width = spectra.shape
    trials = responses.shape[0]
    length = width // 2
    bins = length // RATE
    block = min(CHAN_BLOCK, chans)
    grid = (chans // block, trials)
    flops = 2 * trials * beams * chans * width * width
    bytes_accessed = 2 * (spectra.size + responses.size + backward.size + trials * beams * chans * bins)
    return pl.pallas_call(
        detect_kernel,
        out_shape=jax.ShapeDtypeStruct((trials, beams, chans // 2, 2 * bins), jnp.bfloat16),
        grid_spec=pltpu.PrefetchScalarGridSpec(
            num_scalar_prefetch=1,
            grid=grid,
            in_specs=[
                pl.BlockSpec((beams, block, width), lambda c, d, cl: (0, c, 0)),
                pl.BlockSpec((1, block, width), lambda c, d, cl: (d, c, 0)),
                pl.BlockSpec((width, width), lambda c, d, cl: (0, 0)),
            ],
            out_specs=pl.BlockSpec((1, beams, block // 2, 2 * bins), lambda c, d, cl: (d, 0, c, 0)),
            scratch_shapes=[pltpu.VMEM((beams * block, 2 * bins), jnp.float32)],
        ),
        compiler_params=pltpu.CompilerParams(
            dimension_semantics=("arbitrary", "arbitrary"), vmem_limit_bytes=48 * 1024 * 1024
        ),
        cost_estimate=pl.CostEstimate(flops=flops, transcendentals=0, bytes_accessed=bytes_accessed),
    )(chirp_len, spectra, responses, backward)


def coords(index, z_count):
    return index // (2 * z_count), (index // 2) % z_count, index % 2


def flat(x_lo, z, core, z_count):
    return (x_lo * z_count + z % z_count) * 2 + core


def moves(count, step):
    z_count = count // 4
    pairs = []
    for index in range(count):
        x_lo, z, core = coords(index, z_count)
        pairs.append((index, step(x_lo, z, core, z_count)))
    return pairs


def gather_spectra(own, count):
    z_count = count // 4
    across = moves(count, lambda x, z, c, n: flat(1 - x, z, c, n))
    up = moves(count, lambda x, z, c, n: flat(x, z + 1, c, n))
    down = moves(count, lambda x, z, c, n: flat(x, z - 1, c, n))
    partner = moves(count, lambda x, z, c, n: flat(x, z, 1 - c, n))
    pair = jnp.stack([own, lax.ppermute(own, "dm", across)])
    from_below = [pair]
    from_above = [pair]
    for _ in range(z_count // 2 - 1):
        from_below.append(lax.ppermute(from_below[-1], "dm", up))
        from_above.append(lax.ppermute(from_above[-1], "dm", down))
    far = jnp.stack(
        [lax.ppermute(from_below[-1][0], "dm", up), lax.ppermute(from_above[-1][1], "dm", down)]
    )
    column = jnp.stack(from_above + [far] + from_below[:0:-1])
    both = jnp.stack([column, lax.ppermute(column, "dm", partner)])
    x_me, z_me, c_me = coords(lax.axis_index("dm"), z_count)
    shard = jnp.arange(count, dtype=jnp.int32)
    x_n, z_n, c_n = coords(shard, z_count)
    rel = ((c_n ^ c_me) * z_count + (z_n - z_me) % z_count) * 2 + (x_n ^ x_me)
    return jnp.take(both.reshape((count,) + own.shape), rel, axis=0)


def shards(voltages, responses, chirp_len):
    chans_local, beams, _, length = voltages.shape
    trials, chans = responses.shape[0], responses.shape[1]
    count = chans // chans_local
    forward, backward = dft_tables(length)
    order = sample_order(length, RATE)
    backward = jnp.concatenate([backward[:, order], backward[:, length + order]], 1)
    local = jnp.dot(
        voltages.reshape(-1, 2 * length), forward, preferred_element_type=jnp.float32
    ).astype(jnp.bfloat16)
    local = local.reshape(chans_local, beams, 2 * length).transpose(1, 0, 2)
    gathered = gather_spectra(local, count)
    spectra = gathered.transpose(1, 0, 2, 3).reshape(beams, chans, 2 * length)
    detected = detect(spectra, responses.reshape(trials, chans, 2 * length), chirp_len, backward)
    flattened = detected.reshape(trials, beams, -1)
    return lax.all_to_all(flattened, "beam", split_axis=1, concat_axis=2, tiled=True)


def solution(mesh):
    placed = (P(("beam", "dm"), None, None, None), P("dm", "beam", None, None), P("dm"))
    return jax.shard_map(
        shards, mesh=mesh, in_specs=placed, out_specs=P("dm", "beam", None), check_vma=False
    )
```

```python
import functools
import math

import jax
import jax.numpy as jnp
from jax import lax
from jax.experimental import pallas as pl
from jax.experimental.pallas import tpu as pltpu
from jax.sharding import PartitionSpec as P

RATE = 4
CHAN_BLOCK = 256


def dft_tables(length):
    sample = jnp.arange(length, dtype=jnp.int32)
    phases = sample[:, None] * sample[None, :] % length
    angles = phases.astype(jnp.float32) * (2.0 * math.pi / length)
    cosine = jnp.cos(angles) / math.sqrt(length)
    sine_part = jnp.sin(angles) / math.sqrt(length)
    forward = jnp.concatenate(
        [jnp.concatenate([cosine, -sine_part], 1), jnp.concatenate([sine_part, cosine], 1)], 0
    )
    backward = jnp.concatenate(
        [jnp.concatenate([cosine, sine_part], 1), jnp.concatenate([-sine_part, cosine], 1)], 0
    )
    return (forward.astype(jnp.bfloat16), backward.astype(jnp.bfloat16))


def sample_order(length, rate):
    pos = jnp.arange(length, dtype=jnp.int32)
    bins = length // rate
    return rate * (pos % bins) + pos // bins


def detect_kernel(chirp_ref, table_ref, swap_ref, mine_ref, theirs_ref, resp_ref, back_ref, out_ref, pair_ref):
    _, beams, chans_local, width = mine_ref.shape
    trials = resp_ref.shape[0]
    length = width // 2
    bins = length // RATE
    chans = 2 * chans_local
    keep = swap_ref[0] == 0
    mine = mine_ref[0]
    theirs = theirs_ref[0]
    x = jnp.concatenate([jnp.where(keep, mine, theirs), jnp.where(keep, theirs, mine)], axis=1)
    xr = x[:, :, :length].astype(jnp.float32)
    xi = x[:, :, length:].astype(jnp.float32)
    back = back_ref[...]
    pos = lax.broadcasted_iota(jnp.int32, (1, length), 1)
    t = RATE * (pos % bins) + pos // bins
    lane = lax.broadcasted_iota(jnp.int32, (1, 2 * bins), 1)
    rows = beams * chans // 2
    for d in range(trials):
        h = resp_ref[d]
        hr = h[:, :length].astype(jnp.float32)[None]
        hi = h[:, length:].astype(jnp.float32)[None]
        fr = hr * xr - hi * xi
        fi = hr * xi + hi * xr
        joined = jnp.concatenate([fr, fi], -1).reshape(beams * chans, width).astype(jnp.bfloat16)
        series = jnp.dot(joined, back, preferred_element_type=jnp.float32)
        powers = series[:, :length] ** 2 + series[:, length:] ** 2
        powers = jnp.where(t >= chirp_ref[d], powers, jnp.float32(0.0))
        half = powers[:, : length // 2] + powers[:, length // 2 :]
        pair_ref[...] = half + pltpu.roll(half, bins, 1)
        even = pair_ref[pl.ds(0, rows, stride=2), :]
        odd = pair_ref[pl.ds(1, rows, stride=2), :]
        both = jnp.where(lane < bins, even, odd) / RATE
        out_ref[d] = both.reshape(beams, chans // 2, 2 * bins).astype(out_ref.dtype)


def detect(table, swap, mine, theirs, responses, chirp_len, backward):
    blocks, beams, chans_local, width = mine.shape
    trials, chans = responses.shape[0], responses.shape[1]
    length = width // 2
    bins = length // RATE
    step = 2 * chans_local
    flops = 2 * trials * beams * chans * width * width
    bytes_accessed = 2 * (2 * mine.size + responses.size + backward.size + trials * beams * chans * bins)
    return pl.pallas_call(
        detect_kernel,
        out_shape=jax.ShapeDtypeStruct((trials, beams, chans // 2, 2 * bins), jnp.bfloat16),
        grid_spec=pltpu.PrefetchScalarGridSpec(
            num_scalar_prefetch=3,
            grid=(chans // step,),
            in_specs=[
                pl.BlockSpec((1, beams, chans_local, width), lambda n, cl, tb, sw: (tb[n], 0, 0, 0)),
                pl.BlockSpec((1, beams, chans_local, width), lambda n, cl, tb, sw: (tb[n], 0, 0, 0)),
                pl.BlockSpec((trials, step, width), lambda n, cl, tb, sw: (0, n, 0)),
                pl.BlockSpec((width, width), lambda n, cl, tb, sw: (0, 0)),
            ],
            out_specs=pl.BlockSpec(
                (trials, beams, step // 2, 2 * bins), lambda n, cl, tb, sw: (0, 0, n, 0)
            ),
            scratch_shapes=[pltpu.VMEM((beams * step, 2 * bins), jnp.float32)],
        ),
        compiler_params=pltpu.CompilerParams(
            dimension_semantics=("arbitrary",), vmem_limit_bytes=48 * 1024 * 1024
        ),
        cost_estimate=pl.CostEstimate(flops=flops, transcendentals=0, bytes_accessed=bytes_accessed),
    )(chirp_len, table, swap, mine, theirs, responses, backward)


def coords(index, z_count):
    return index // (2 * z_count), (index // 2) % z_count, index % 2


def flat(x_lo, z, core, z_count):
    return (x_lo * z_count + z % z_count) * 2 + core


def moves(count, step):
    z_count = count // 4
    pairs = []
    for index in range(count):
        x_lo, z, core = coords(index, z_count)
        pairs.append((index, step(x_lo, z, core, z_count)))
    return pairs


def gather_spectra(own, count):
    z_count = count // 4
    across = moves(count, lambda x, z, c, n: flat(1 - x, z, c, n))
    up = moves(count, lambda x, z, c, n: flat(x, z + 1, c, n))
    down = moves(count, lambda x, z, c, n: flat(x, z - 1, c, n))
    partner = moves(count, lambda x, z, c, n: flat(x, z, 1 - c, n))
    pair = jnp.stack([own, lax.ppermute(own, "dm", across)])
    from_below = [pair]
    from_above = [pair]
    for _ in range(z_count // 2 - 1):
        from_below.append(lax.ppermute(from_below[-1], "dm", up))
        from_above.append(lax.ppermute(from_above[-1], "dm", down))
    far = jnp.stack(
        [lax.ppermute(from_below[-1][0], "dm", up), lax.ppermute(from_above[-1][1], "dm", down)]
    )
    column = jnp.stack(from_above + [far] + from_below[:0:-1])
    column = column.reshape((2 * z_count,) + own.shape)
    return column, lax.ppermute(column, "dm", partner)


def shards(voltages, responses, chirp_len):
    chans_local, beams, _, length = voltages.shape
    trials, chans = responses.shape[0], responses.shape[1]
    count = chans // chans_local
    z_count = count // 4
    forward, backward = dft_tables(length)
    order = sample_order(length, RATE)
    backward = jnp.concatenate([backward[:, order], backward[:, length + order]], 1)
    local = jnp.dot(
        voltages.reshape(-1, 2 * length), forward, preferred_element_type=jnp.float32
    ).astype(jnp.bfloat16)
    local = local.reshape(chans_local, beams, 2 * length).transpose(1, 0, 2)
    mine, theirs = gather_spectra(local, count)
    x_me, z_me, c_me = coords(lax.axis_index("dm"), z_count)
    block = jnp.arange(count // 2, dtype=jnp.int32)
    table = ((block % z_count - z_me) % z_count) * 2 + ((block // z_count) ^ x_me)
    swap = jnp.reshape(c_me, (1,)).astype(jnp.int32)
    detected = detect(
        table, swap, mine, theirs, responses.reshape(trials, chans, 2 * length), chirp_len, backward
    )
    flattened = detected.reshape(trials, beams, -1)
    return lax.all_to_all(flattened, "beam", split_axis=1, concat_axis=2, tiled=True)


def solution(mesh):
    placed = (P(("beam", "dm"), None, None, None), P("dm", "beam", None, None), P("dm"))
    return jax.shard_map(
        shards, mesh=mesh, in_specs=placed, out_specs=P("dm", "beam", None), check_vma=False
    )
```

```python
import functools
import math

import jax
import jax.numpy as jnp
from jax import lax
from jax.experimental import pallas as pl
from jax.experimental.pallas import tpu as pltpu
from jax.sharding import PartitionSpec as P

RATE = 4
CHAN_BLOCK = 256


def dft_tables(length):
    sample = jnp.arange(length, dtype=jnp.int32)
    phases = sample[:, None] * sample[None, :] % length
    angles = phases.astype(jnp.float32) * (2.0 * math.pi / length)
    cosine = jnp.cos(angles) / math.sqrt(length)
    sine_part = jnp.sin(angles) / math.sqrt(length)
    forward = jnp.concatenate(
        [jnp.concatenate([cosine, -sine_part], 1), jnp.concatenate([sine_part, cosine], 1)], 0
    )
    backward = jnp.concatenate(
        [jnp.concatenate([cosine, sine_part], 1), jnp.concatenate([-sine_part, cosine], 1)], 0
    )
    return (forward.astype(jnp.bfloat16), backward.astype(jnp.bfloat16))


def sample_order(length, rate):
    pos = jnp.arange(length, dtype=jnp.int32)
    bins = length // rate
    return rate * (pos % bins) + pos // bins


def detect_kernel(chirp_ref, table_ref, swap_ref, mine_ref, theirs_ref, resp_ref, back_ref, out_ref, pair_ref):
    _, beams, chans_local, width = mine_ref.shape
    trials = resp_ref.shape[0]
    length = width // 2
    bins = length // RATE
    chans = 2 * chans_local
    keep = swap_ref[0] == 0
    mine = mine_ref[0]
    theirs = theirs_ref[0]
    x = jnp.concatenate([jnp.where(keep, mine, theirs), jnp.where(keep, theirs, mine)], axis=1)
    xr = x[:, :, :length].astype(jnp.float32)
    xi = x[:, :, length:].astype(jnp.float32)
    back = back_ref[...]
    pos = lax.broadcasted_iota(jnp.int32, (1, length), 1)
    t = RATE * (pos % bins) + pos // bins
    lane = lax.broadcasted_iota(jnp.int32, (1, 2 * bins), 1)
    rows = beams * chans // 2
    for d in range(trials):
        h = resp_ref[d]
        hr = h[:, :length].astype(jnp.float32)[None]
        hi = h[:, length:].astype(jnp.float32)[None]
        fr = hr * xr - hi * xi
        fi = hr * xi + hi * xr
        joined = jnp.concatenate([fr, fi], -1).reshape(beams * chans, width).astype(jnp.bfloat16)
        series = jnp.dot(joined, back, preferred_element_type=jnp.float32)
        powers = series[:, :length] ** 2 + series[:, length:] ** 2
        powers = jnp.where(t >= chirp_ref[d], powers, jnp.float32(0.0))
        half = powers[:, : length // 2] + powers[:, length // 2 :]
        pair_ref[...] = half + pltpu.roll(half, bins, 1)
        even = pair_ref[pl.ds(0, rows, stride=2), :]
        odd = pair_ref[pl.ds(1, rows, stride=2), :]
        both = jnp.where(lane < bins, even, odd) / RATE
        out_ref[:, d] = both.reshape(beams, chans // 2, 2 * bins).astype(out_ref.dtype)


def detect(table, swap, mine, theirs, responses, chirp_len, backward):
    blocks, beams, chans_local, width = mine.shape
    trials, chans = responses.shape[0], responses.shape[1]
    length = width // 2
    bins = length // RATE
    step = 2 * chans_local
    flops = 2 * trials * beams * chans * width * width
    bytes_accessed = 2 * (2 * mine.size + responses.size + backward.size + trials * beams * chans * bins)
    return pl.pallas_call(
        detect_kernel,
        out_shape=jax.ShapeDtypeStruct((beams, trials, chans // 2, 2 * bins), jnp.bfloat16),
        grid_spec=pltpu.PrefetchScalarGridSpec(
            num_scalar_prefetch=3,
            grid=(chans // step,),
            in_specs=[
                pl.BlockSpec((1, beams, chans_local, width), lambda n, cl, tb, sw: (tb[n], 0, 0, 0)),
                pl.BlockSpec((1, beams, chans_local, width), lambda n, cl, tb, sw: (tb[n], 0, 0, 0)),
                pl.BlockSpec((trials, step, width), lambda n, cl, tb, sw: (0, n, 0)),
                pl.BlockSpec((width, width), lambda n, cl, tb, sw: (0, 0)),
            ],
            out_specs=pl.BlockSpec(
                (beams, trials, step // 2, 2 * bins), lambda n, cl, tb, sw: (0, 0, n, 0)
            ),
            scratch_shapes=[pltpu.VMEM((beams * step, 2 * bins), jnp.float32)],
        ),
        compiler_params=pltpu.CompilerParams(
            dimension_semantics=("arbitrary",), vmem_limit_bytes=48 * 1024 * 1024
        ),
        cost_estimate=pl.CostEstimate(flops=flops, transcendentals=0, bytes_accessed=bytes_accessed),
    )(chirp_len, table, swap, mine, theirs, responses, backward)


def coords(index, z_count):
    return index // (2 * z_count), (index // 2) % z_count, index % 2


def flat(x_lo, z, core, z_count):
    return (x_lo * z_count + z % z_count) * 2 + core


def moves(count, step):
    z_count = count // 4
    pairs = []
    for index in range(count):
        x_lo, z, core = coords(index, z_count)
        pairs.append((index, step(x_lo, z, core, z_count)))
    return pairs


def gather_spectra(own, count):
    z_count = count // 4
    across = moves(count, lambda x, z, c, n: flat(1 - x, z, c, n))
    up = moves(count, lambda x, z, c, n: flat(x, z + 1, c, n))
    down = moves(count, lambda x, z, c, n: flat(x, z - 1, c, n))
    partner = moves(count, lambda x, z, c, n: flat(x, z, 1 - c, n))
    pair = jnp.stack([own, lax.ppermute(own, "dm", across)])
    from_below = [pair]
    from_above = [pair]
    for _ in range(z_count // 2 - 1):
        from_below.append(lax.ppermute(from_below[-1], "dm", up))
        from_above.append(lax.ppermute(from_above[-1], "dm", down))
    far = jnp.stack(
        [lax.ppermute(from_below[-1][0], "dm", up), lax.ppermute(from_above[-1][1], "dm", down)]
    )
    column = jnp.stack(from_above + [far] + from_below[:0:-1])
    column = column.reshape((2 * z_count,) + own.shape)
    return column, lax.ppermute(column, "dm", partner)


def shards(voltages, responses, chirp_len):
    chans_local, beams, _, length = voltages.shape
    trials, chans = responses.shape[0], responses.shape[1]
    count = chans // chans_local
    z_count = count // 4
    forward, backward = dft_tables(length)
    order = sample_order(length, RATE)
    backward = jnp.concatenate([backward[:, order], backward[:, length + order]], 1)
    local = jnp.dot(
        voltages.reshape(-1, 2 * length), forward, preferred_element_type=jnp.float32
    ).astype(jnp.bfloat16)
    local = local.reshape(chans_local, beams, 2 * length).transpose(1, 0, 2)
    resp = responses.reshape(trials, chans, 2 * length)
    local, resp, backward = lax.optimization_barrier((local, resp, backward))
    mine, theirs = gather_spectra(local, count)
    x_me, z_me, c_me = coords(lax.axis_index("dm"), z_count)
    block = jnp.arange(count // 2, dtype=jnp.int32)
    table = ((block % z_count - z_me) % z_count) * 2 + ((block // z_count) ^ x_me)
    swap = jnp.reshape(c_me, (1,)).astype(jnp.int32)
    detected = detect(table, swap, mine, theirs, resp, chirp_len, backward)
    return exchange_beams(detected.reshape(beams, trials, -1))[:, None]


def exchange_beams(detected):
    beams = detected.shape[0]
    me = lax.axis_index("beam")
    pieces = [lax.dynamic_index_in_dim(detected, me, 0, keepdims=False)]
    for shift in range(1, beams):
        part = lax.dynamic_index_in_dim(detected, (me + shift) % beams, 0, keepdims=False)
        pieces.append(lax.ppermute(part, "beam", [(b, (b + shift) % beams) for b in range(beams)]))
    stacked = jnp.stack(pieces[:1] + pieces[:0:-1])
    doubled = jnp.concatenate([stacked, stacked], 0)
    ordered = lax.dynamic_slice_in_dim(doubled, (beams - me) % beams, beams, 0)
    return ordered.transpose(1, 0, 2).reshape(detected.shape[1], -1)


def solution(mesh):
    placed = (P(("beam", "dm"), None, None, None), P("dm", "beam", None, None), P("dm"))
    return jax.shard_map(
        shards, mesh=mesh, in_specs=placed, out_specs=P("dm", "beam", None), check_vma=False
    )
```

```python
import functools
import math

import jax
import jax.numpy as jnp
from jax import lax
from jax.experimental import pallas as pl
from jax.experimental.pallas import tpu as pltpu
from jax.sharding import PartitionSpec as P

RATE = 4
CHAN_BLOCK = 256


def dft_tables(length):
    sample = jnp.arange(length, dtype=jnp.int32)
    phases = sample[:, None] * sample[None, :] % length
    angles = phases.astype(jnp.float32) * (2.0 * math.pi / length)
    cosine = jnp.cos(angles) / math.sqrt(length)
    sine_part = jnp.sin(angles) / math.sqrt(length)
    forward = jnp.concatenate(
        [jnp.concatenate([cosine, -sine_part], 1), jnp.concatenate([sine_part, cosine], 1)], 0
    )
    backward = jnp.concatenate(
        [jnp.concatenate([cosine, sine_part], 1), jnp.concatenate([-sine_part, cosine], 1)], 0
    )
    return (forward.astype(jnp.bfloat16), backward.astype(jnp.bfloat16))


def sample_order(length, rate):
    pos = jnp.arange(length, dtype=jnp.int32)
    bins = length // rate
    return rate * (pos % bins) + pos // bins


def detect_kernel(chirp_ref, table_ref, swap_ref, mine_ref, theirs_ref, resp_ref, back_ref, out_ref, pair_ref):
    _, beams, chans_local, width = mine_ref.shape
    trials = resp_ref.shape[0]
    length = width // 2
    bins = length // RATE
    chans = 2 * chans_local
    keep = swap_ref[0] == 0
    mine = mine_ref[0]
    theirs = theirs_ref[0]
    x = jnp.concatenate([jnp.where(keep, mine, theirs), jnp.where(keep, theirs, mine)], axis=1)
    xr = x[:, :, :length].astype(jnp.float32)
    xi = x[:, :, length:].astype(jnp.float32)
    back = back_ref[...]
    pos = lax.broadcasted_iota(jnp.int32, (1, length), 1)
    t = RATE * (pos % bins) + pos // bins
    lane = lax.broadcasted_iota(jnp.int32, (1, 2 * bins), 1)
    rows = beams * chans // 2
    for d in range(trials):
        h = resp_ref[d]
        hr = h[:, :length].astype(jnp.float32)[None]
        hi = h[:, length:].astype(jnp.float32)[None]
        fr = hr * xr - hi * xi
        fi = hr * xi + hi * xr
        joined = jnp.concatenate([fr, fi], -1).reshape(beams * chans, width).astype(jnp.bfloat16)
        series = jnp.dot(joined, back, preferred_element_type=jnp.float32)
        powers = series[:, :length] ** 2 + series[:, length:] ** 2
        powers = jnp.where(t >= chirp_ref[d], powers, jnp.float32(0.0))
        half = powers[:, : length // 2] + powers[:, length // 2 :]
        pair_ref[...] = half + pltpu.roll(half, bins, 1)
        even = pair_ref[pl.ds(0, rows, stride=2), :]
        odd = pair_ref[pl.ds(1, rows, stride=2), :]
        both = jnp.where(lane < bins, even, odd) / RATE
        out_ref[d] = both.reshape(beams, chans // 2, 2 * bins).astype(out_ref.dtype)


def detect(table, swap, mine, theirs, responses, chirp_len, backward):
    blocks, beams, chans_local, width = mine.shape
    trials = responses.shape[0]
    length = width // 2
    bins = length // RATE
    step = 2 * chans_local
    flops = 2 * trials * beams * blocks * step * width * width
    bytes_accessed = 2 * (2 * mine.size + blocks * (trials * step * width + trials * beams * step * bins))
    return pl.pallas_call(
        detect_kernel,
        out_shape=jax.ShapeDtypeStruct((trials, beams, blocks * step // 2, 2 * bins), jnp.bfloat16),
        grid_spec=pltpu.PrefetchScalarGridSpec(
            num_scalar_prefetch=3,
            grid=(blocks,),
            in_specs=[
                pl.BlockSpec((1, beams, chans_local, width), lambda n, cl, tb, sw: (n, 0, 0, 0)),
                pl.BlockSpec((1, beams, chans_local, width), lambda n, cl, tb, sw: (n, 0, 0, 0)),
                pl.BlockSpec((trials, step, width), lambda n, cl, tb, sw: (0, tb[n], 0)),
                pl.BlockSpec((width, width), lambda n, cl, tb, sw: (0, 0)),
            ],
            out_specs=pl.BlockSpec(
                (trials, beams, step // 2, 2 * bins), lambda n, cl, tb, sw: (0, 0, n, 0)
            ),
            scratch_shapes=[pltpu.VMEM((beams * step, 2 * bins), jnp.float32)],
        ),
        compiler_params=pltpu.CompilerParams(
            dimension_semantics=("arbitrary",), vmem_limit_bytes=48 * 1024 * 1024
        ),
        cost_estimate=pl.CostEstimate(flops=flops, transcendentals=0, bytes_accessed=bytes_accessed),
    )(chirp_len, table, swap, mine, theirs, responses, backward)


def coords(index, z_count):
    return index // (2 * z_count), (index // 2) % z_count, index % 2


def flat(x_lo, z, core, z_count):
    return (x_lo * z_count + z % z_count) * 2 + core


def moves(count, step):
    z_count = count // 4
    pairs = []
    for index in range(count):
        x_lo, z, core = coords(index, z_count)
        pairs.append((index, step(x_lo, z, core, z_count)))
    return pairs


def gather_columns(own, count):
    z_count = count // 4
    across = moves(count, lambda x, z, c, n: flat(1 - x, z, c, n))
    up = moves(count, lambda x, z, c, n: flat(x, z + 1, c, n))
    down = moves(count, lambda x, z, c, n: flat(x, z - 1, c, n))
    pair = jnp.stack([own, lax.ppermute(own, "dm", across)])
    from_below = [pair]
    from_above = [pair]
    for _ in range(z_count // 2 - 1):
        from_below.append(lax.ppermute(from_below[-1], "dm", up))
        from_above.append(lax.ppermute(from_above[-1], "dm", down))
    far = jnp.stack(
        [lax.ppermute(from_below[-1][0], "dm", up), lax.ppermute(from_above[-1][1], "dm", down)]
    )
    near_count = z_count // 4 + 1
    near = from_above[:near_count] + from_below[1:near_count]
    near_offsets = list(range(near_count)) + [-k for k in range(1, near_count)]
    rest = from_above[near_count:] + [far] + from_below[near_count:]
    rest_offsets = list(range(near_count, z_count // 2)) + [z_count // 2] + [
        -k for k in range(near_count, z_count // 2)
    ]
    chunks = []
    for offsets, pieces in ((near_offsets, near), (rest_offsets, rest)):
        chunks.append((offsets, jnp.stack(pieces).reshape((2 * len(pieces),) + own.shape)))
    return chunks


def shards(voltages, responses, chirp_len):
    chans_local, beams, _, length = voltages.shape
    trials, chans = responses.shape[0], responses.shape[1]
    count = chans // chans_local
    z_count = count // 4
    forward, backward = dft_tables(length)
    order = sample_order(length, RATE)
    backward = jnp.concatenate([backward[:, order], backward[:, length + order]], 1)
    local = jnp.dot(
        voltages.reshape(-1, 2 * length), forward, preferred_element_type=jnp.float32
    ).astype(jnp.bfloat16)
    local = local.reshape(chans_local, beams, 2 * length).transpose(1, 0, 2)
    resp = responses.reshape(trials, chans, 2 * length)
    x_me, z_me, c_me = coords(lax.axis_index("dm"), z_count)
    swap = jnp.reshape(c_me, (1,)).astype(jnp.int32)
    partner = moves(count, lambda x, z, c, n: flat(x, z, 1 - c, n))
    outputs = []
    naturals = []
    for offsets, mine in gather_columns(local, count):
        theirs = lax.ppermute(mine, "dm", partner)
        offs = jnp.array(offsets, dtype=jnp.int32)[:, None]
        x_rel = jnp.arange(2, dtype=jnp.int32)[None, :]
        natural = ((x_rel ^ x_me) * z_count + (z_me + offs) % z_count).reshape(-1)
        detected = detect(natural, swap, mine, theirs, resp, chirp_len, backward)
        flattened = detected.reshape(trials, beams, -1)
        moved = lax.all_to_all(flattened, "beam", split_axis=1, concat_axis=2, tiled=True)
        outputs.append(moved.reshape(trials, beams, natural.shape[0], -1))
        naturals.append(natural)
    natural = jnp.concatenate(naturals)
    place = jnp.zeros_like(natural).at[natural].set(jnp.arange(natural.shape[0], dtype=jnp.int32))
    joined = jnp.take(jnp.concatenate(outputs, 2), place, axis=2)
    return joined.reshape(trials, 1, -1)


def solution(mesh):
    placed = (P(("beam", "dm"), None, None, None), P("dm", "beam", None, None), P("dm"))
    return jax.shard_map(
        shards, mesh=mesh, in_specs=placed, out_specs=P("dm", "beam", None), check_vma=False
    )
```

```python
import functools
import math

import jax
import jax.numpy as jnp
from jax import lax
from jax.experimental import pallas as pl
from jax.experimental.pallas import tpu as pltpu
from jax.sharding import PartitionSpec as P

RATE = 4
CHAN_BLOCK = 256


def dft_tables(length):
    sample = jnp.arange(length, dtype=jnp.int32)
    phases = sample[:, None] * sample[None, :] % length
    angles = phases.astype(jnp.float32) * (2.0 * math.pi / length)
    cosine = jnp.cos(angles) / math.sqrt(length)
    sine_part = jnp.sin(angles) / math.sqrt(length)
    forward = jnp.concatenate(
        [jnp.concatenate([cosine, -sine_part], 1), jnp.concatenate([sine_part, cosine], 1)], 0
    )
    backward = jnp.concatenate(
        [jnp.concatenate([cosine, sine_part], 1), jnp.concatenate([-sine_part, cosine], 1)], 0
    )
    return (forward.astype(jnp.bfloat16), backward.astype(jnp.bfloat16))


def sample_order(length, rate):
    pos = jnp.arange(length, dtype=jnp.int32)
    bins = length // rate
    return rate * (pos % bins) + pos // bins


def detect_kernel(chirp_ref, table_ref, swap_ref, mine_ref, theirs_ref, resp_ref, back_ref, out_ref, pair_ref):
    _, beams, chans_local, width = mine_ref.shape
    trials = resp_ref.shape[0]
    length = width // 2
    bins = length // RATE
    chans = 2 * chans_local
    keep = swap_ref[0] == 0
    mine = mine_ref[0]
    theirs = theirs_ref[0]
    x = jnp.concatenate([jnp.where(keep, mine, theirs), jnp.where(keep, theirs, mine)], axis=1)
    xr = x[:, :, :length].astype(jnp.float32)
    xi = x[:, :, length:].astype(jnp.float32)
    back = back_ref[...]
    pos = lax.broadcasted_iota(jnp.int32, (1, length), 1)
    t = RATE * (pos % bins) + pos // bins
    lane = lax.broadcasted_iota(jnp.int32, (1, 2 * bins), 1)
    rows = beams * chans // 2
    for d in range(trials):
        h = resp_ref[d]
        hr = h[:, :length].astype(jnp.float32)[None]
        hi = h[:, length:].astype(jnp.float32)[None]
        fr = hr * xr - hi * xi
        fi = hr * xi + hi * xr
        joined = jnp.concatenate([fr, fi], -1).reshape(beams * chans, width).astype(jnp.bfloat16)
        series = jnp.dot(joined, back, preferred_element_type=jnp.float32)
        powers = series[:, :length] ** 2 + series[:, length:] ** 2
        powers = jnp.where(t >= chirp_ref[d], powers, jnp.float32(0.0))
        half = powers[:, : length // 2] + powers[:, length // 2 :]
        pair_ref[...] = half + pltpu.roll(half, bins, 1)
        even = pair_ref[pl.ds(0, rows, stride=2), :]
        odd = pair_ref[pl.ds(1, rows, stride=2), :]
        both = jnp.where(lane < bins, even, odd) / RATE
        out_ref[d] = both.reshape(beams, chans // 2, 2 * bins).astype(out_ref.dtype)


def detect(table, swap, mine, theirs, responses, chirp_len, backward, first, count):
    blocks, beams, chans_local, width = mine.shape
    trials, chans = responses.shape[0], responses.shape[1]
    length = width // 2
    bins = length // RATE
    step = 2 * chans_local
    chans = count * step
    flops = 2 * trials * beams * chans * width * width
    bytes_accessed = 2 * (chans * beams * width + trials * chans * width + trials * beams * chans * bins)
    return pl.pallas_call(
        detect_kernel,
        out_shape=jax.ShapeDtypeStruct((trials, beams, chans // 2, 2 * bins), jnp.bfloat16),
        grid_spec=pltpu.PrefetchScalarGridSpec(
            num_scalar_prefetch=3,
            grid=(count,),
            in_specs=[
                pl.BlockSpec((1, beams, chans_local, width), lambda n, cl, tb, sw: (tb[n + first], 0, 0, 0)),
                pl.BlockSpec((1, beams, chans_local, width), lambda n, cl, tb, sw: (tb[n + first], 0, 0, 0)),
                pl.BlockSpec((trials, step, width), lambda n, cl, tb, sw: (0, n + first, 0)),
                pl.BlockSpec((width, width), lambda n, cl, tb, sw: (0, 0)),
            ],
            out_specs=pl.BlockSpec(
                (trials, beams, step // 2, 2 * bins), lambda n, cl, tb, sw: (0, 0, n, 0)
            ),
            scratch_shapes=[pltpu.VMEM((beams * step, 2 * bins), jnp.float32)],
        ),
        compiler_params=pltpu.CompilerParams(
            dimension_semantics=("arbitrary",), vmem_limit_bytes=48 * 1024 * 1024
        ),
        cost_estimate=pl.CostEstimate(flops=flops, transcendentals=0, bytes_accessed=bytes_accessed),
    )(chirp_len, table, swap, mine, theirs, responses, backward)


def coords(index, z_count):
    return index // (2 * z_count), (index // 2) % z_count, index % 2


def flat(x_lo, z, core, z_count):
    return (x_lo * z_count + z % z_count) * 2 + core


def moves(count, step):
    z_count = count // 4
    pairs = []
    for index in range(count):
        x_lo, z, core = coords(index, z_count)
        pairs.append((index, step(x_lo, z, core, z_count)))
    return pairs


def gather_spectra(own, count):
    z_count = count // 4
    across = moves(count, lambda x, z, c, n: flat(1 - x, z, c, n))
    up = moves(count, lambda x, z, c, n: flat(x, z + 1, c, n))
    down = moves(count, lambda x, z, c, n: flat(x, z - 1, c, n))
    partner = moves(count, lambda x, z, c, n: flat(x, z, 1 - c, n))
    pair = jnp.stack([own, lax.ppermute(own, "dm", across)])
    from_below = [pair]
    from_above = [pair]
    for _ in range(z_count // 2 - 1):
        from_below.append(lax.ppermute(from_below[-1], "dm", up))
        from_above.append(lax.ppermute(from_above[-1], "dm", down))
    far = jnp.stack(
        [lax.ppermute(from_below[-1][0], "dm", up), lax.ppermute(from_above[-1][1], "dm", down)]
    )
    column = jnp.stack(from_above + [far] + from_below[:0:-1])
    column = column.reshape((2 * z_count,) + own.shape)
    return column, lax.ppermute(column, "dm", partner)


def shards(voltages, responses, chirp_len):
    chans_local, beams, _, length = voltages.shape
    trials, chans = responses.shape[0], responses.shape[1]
    count = chans // chans_local
    z_count = count // 4
    forward, backward = dft_tables(length)
    order = sample_order(length, RATE)
    backward = jnp.concatenate([backward[:, order], backward[:, length + order]], 1)
    local = jnp.dot(
        voltages.reshape(-1, 2 * length), forward, preferred_element_type=jnp.float32
    ).astype(jnp.bfloat16)
    local = local.reshape(chans_local, beams, 2 * length).transpose(1, 0, 2)
    mine, theirs = gather_spectra(local, count)
    x_me, z_me, c_me = coords(lax.axis_index("dm"), z_count)
    block = jnp.arange(count // 2, dtype=jnp.int32)
    table = ((block % z_count - z_me) % z_count) * 2 + ((block // z_count) ^ x_me)
    swap = jnp.reshape(c_me, (1,)).astype(jnp.int32)
    resp = responses.reshape(trials, chans, 2 * length)
    halves = []
    blocks = count // 2
    for first in (0, blocks // 2):
        detected = detect(table, swap, mine, theirs, resp, chirp_len, backward, first, blocks // 2)
        flattened = detected.reshape(trials, beams, -1)
        moved = lax.all_to_all(flattened, "beam", split_axis=1, concat_axis=2, tiled=True)
        halves.append(moved.reshape(trials, beams, 1, -1))
    return jnp.concatenate(halves, 2).reshape(trials, 1, -1)


def solution(mesh):
    placed = (P(("beam", "dm"), None, None, None), P("dm", "beam", None, None), P("dm"))
    return jax.shard_map(
        shards, mesh=mesh, in_specs=placed, out_specs=P("dm", "beam", None), check_vma=False
    )
```

```python
import functools
import math

import jax
import jax.numpy as jnp
from jax import lax
from jax.experimental import pallas as pl
from jax.experimental.pallas import tpu as pltpu
from jax.sharding import PartitionSpec as P

RATE = 4
CHAN_BLOCK = 256


def dft_tables(length):
    sample = jnp.arange(length, dtype=jnp.int32)
    phases = sample[:, None] * sample[None, :] % length
    angles = phases.astype(jnp.float32) * (2.0 * math.pi / length)
    cosine = jnp.cos(angles) / math.sqrt(length)
    sine_part = jnp.sin(angles) / math.sqrt(length)
    forward = jnp.concatenate(
        [jnp.concatenate([cosine, -sine_part], 1), jnp.concatenate([sine_part, cosine], 1)], 0
    )
    backward = jnp.concatenate(
        [jnp.concatenate([cosine, sine_part], 1), jnp.concatenate([-sine_part, cosine], 1)], 0
    )
    return (forward.astype(jnp.bfloat16), backward.astype(jnp.bfloat16))


def sample_order(length, rate):
    pos = jnp.arange(length, dtype=jnp.int32)
    bins = length // rate
    return rate * (pos % bins) + pos // bins


def detect_kernel(chirp_ref, table_ref, swap_ref, mine_ref, theirs_ref, resp_ref, back_ref, out_ref, pair_ref):
    _, beams, chans_local, width = mine_ref.shape
    trials = resp_ref.shape[0]
    length = width // 2
    bins = length // RATE
    chans = 2 * chans_local
    keep = swap_ref[0] == 0
    mine = mine_ref[0]
    theirs = theirs_ref[0]
    x = jnp.concatenate([jnp.where(keep, mine, theirs), jnp.where(keep, theirs, mine)], axis=1)
    xr = x[:, :, :length].astype(jnp.float32)
    xi = x[:, :, length:].astype(jnp.float32)
    back = back_ref[...]
    pos = lax.broadcasted_iota(jnp.int32, (1, length), 1)
    t = RATE * (pos % bins) + pos // bins
    lane = lax.broadcasted_iota(jnp.int32, (1, 2 * bins), 1)
    rows = beams * chans // 2
    for d in range(trials):
        h = resp_ref[d]
        hr = h[:, :length].astype(jnp.float32)[None]
        hi = h[:, length:].astype(jnp.float32)[None]
        fr = hr * xr - hi * xi
        fi = hr * xi + hi * xr
        joined = jnp.concatenate([fr, fi], -1).reshape(beams * chans, width).astype(jnp.bfloat16)
        series = jnp.dot(joined, back, preferred_element_type=jnp.float32)
        powers = series[:, :length] ** 2 + series[:, length:] ** 2
        powers = jnp.where(t >= chirp_ref[d], powers, jnp.float32(0.0))
        half = powers[:, : length // 2] + powers[:, length // 2 :]
        pair_ref[...] = half + pltpu.roll(half, bins, 1)
        even = pair_ref[pl.ds(0, rows, stride=2), :]
        odd = pair_ref[pl.ds(1, rows, stride=2), :]
        both = jnp.where(lane < bins, even, odd) / RATE
        out_ref[:, d] = both.reshape(beams, chans // 2, 2 * bins).astype(out_ref.dtype)


def detect(table, swap, mine, theirs, responses, chirp_len, backward):
    blocks, beams, chans_local, width = mine.shape
    trials, chans = responses.shape[0], responses.shape[1]
    length = width // 2
    bins = length // RATE
    step = 2 * chans_local
    flops = 2 * trials * beams * chans * width * width
    bytes_accessed = 2 * (2 * mine.size + responses.size + backward.size + trials * beams * chans * bins)
    return pl.pallas_call(
        detect_kernel,
        out_shape=jax.ShapeDtypeStruct((beams, trials, chans // 2, 2 * bins), jnp.bfloat16),
        grid_spec=pltpu.PrefetchScalarGridSpec(
            num_scalar_prefetch=3,
            grid=(chans // step,),
            in_specs=[
                pl.BlockSpec((1, beams, chans_local, width), lambda n, cl, tb, sw: (tb[n], 0, 0, 0)),
                pl.BlockSpec((1, beams, chans_local, width), lambda n, cl, tb, sw: (tb[n], 0, 0, 0)),
                pl.BlockSpec((trials, step, width), lambda n, cl, tb, sw: (0, n, 0)),
                pl.BlockSpec((width, width), lambda n, cl, tb, sw: (0, 0)),
            ],
            out_specs=pl.BlockSpec(
                (beams, trials, step // 2, 2 * bins), lambda n, cl, tb, sw: (0, 0, n, 0)
            ),
            scratch_shapes=[pltpu.VMEM((beams * step, 2 * bins), jnp.float32)],
        ),
        compiler_params=pltpu.CompilerParams(
            dimension_semantics=("arbitrary",), vmem_limit_bytes=48 * 1024 * 1024
        ),
        cost_estimate=pl.CostEstimate(flops=flops, transcendentals=0, bytes_accessed=bytes_accessed),
    )(chirp_len, table, swap, mine, theirs, responses, backward)


def coords(index, z_count):
    return index // (2 * z_count), (index // 2) % z_count, index % 2


def flat(x_lo, z, core, z_count):
    return (x_lo * z_count + z % z_count) * 2 + core


def moves(count, step):
    z_count = count // 4
    pairs = []
    for index in range(count):
        x_lo, z, core = coords(index, z_count)
        pairs.append((index, step(x_lo, z, core, z_count)))
    return pairs


def gather_spectra(own, count):
    z_count = count // 4
    across = moves(count, lambda x, z, c, n: flat(1 - x, z, c, n))
    up = moves(count, lambda x, z, c, n: flat(x, z + 1, c, n))
    down = moves(count, lambda x, z, c, n: flat(x, z - 1, c, n))
    partner = moves(count, lambda x, z, c, n: flat(x, z, 1 - c, n))
    pair = jnp.stack([own, lax.ppermute(own, "dm", across)])
    from_below = [pair]
    from_above = [pair]
    for _ in range(z_count // 2 - 1):
        from_below.append(lax.ppermute(from_below[-1], "dm", up))
        from_above.append(lax.ppermute(from_above[-1], "dm", down))
    far = jnp.stack(
        [lax.ppermute(from_below[-1][0], "dm", up), lax.ppermute(from_above[-1][1], "dm", down)]
    )
    column = jnp.stack(from_above + [far] + from_below[:0:-1])
    column = column.reshape((2 * z_count,) + own.shape)
    return column, lax.ppermute(column, "dm", partner)


def shards(voltages, responses, chirp_len):
    chans_local, beams, _, length = voltages.shape
    trials, chans = responses.shape[0], responses.shape[1]
    count = chans // chans_local
    z_count = count // 4
    forward, backward = dft_tables(length)
    order = sample_order(length, RATE)
    backward = jnp.concatenate([backward[:, order], backward[:, length + order]], 1)
    local = jnp.dot(
        voltages.reshape(-1, 2 * length), forward, preferred_element_type=jnp.float32
    ).astype(jnp.bfloat16)
    local = local.reshape(chans_local, beams, 2 * length).transpose(1, 0, 2)
    mine, theirs = gather_spectra(local, count)
    x_me, z_me, c_me = coords(lax.axis_index("dm"), z_count)
    block = jnp.arange(count // 2, dtype=jnp.int32)
    table = ((block % z_count - z_me) % z_count) * 2 + ((block // z_count) ^ x_me)
    swap = jnp.reshape(c_me, (1,)).astype(jnp.int32)
    detected = detect(
        table, swap, mine, theirs, responses.reshape(trials, chans, 2 * length), chirp_len, backward
    )
    moved = lax.all_to_all(detected.transpose(1, 0, 2, 3), "beam", split_axis=1, concat_axis=2, tiled=True)
    return moved.reshape(trials, 1, -1)


def solution(mesh):
    placed = (P(("beam", "dm"), None, None, None), P("dm", "beam", None, None), P("dm"))
    return jax.shard_map(
        shards, mesh=mesh, in_specs=placed, out_specs=P("dm", "beam", None), check_vma=False
    )
```

```python
import functools
import math

import jax
import ml_dtypes
import numpy as np
import jax.numpy as jnp
from jax import lax
from jax.experimental import pallas as pl
from jax.experimental.pallas import tpu as pltpu
from jax.sharding import PartitionSpec as P

RATE = 4
CHAN_BLOCK = 256


def dft_tables(length):
    sample = jnp.arange(length, dtype=jnp.int32)
    phases = sample[:, None] * sample[None, :] % length
    angles = phases.astype(jnp.float32) * (2.0 * math.pi / length)
    cosine = jnp.cos(angles) / math.sqrt(length)
    sine_part = jnp.sin(angles) / math.sqrt(length)
    forward = jnp.concatenate(
        [jnp.concatenate([cosine, -sine_part], 1), jnp.concatenate([sine_part, cosine], 1)], 0
    )
    backward = jnp.concatenate(
        [jnp.concatenate([cosine, sine_part], 1), jnp.concatenate([-sine_part, cosine], 1)], 0
    )
    return (forward.astype(jnp.bfloat16), backward.astype(jnp.bfloat16))


def constant_tables(length, rate):
    sample = np.arange(length, dtype=np.int32)
    phases = sample[:, None] * sample[None, :] % length
    angles = phases.astype(np.float32) * np.float32(2.0 * math.pi / length)
    cosine = np.cos(angles) / np.float32(math.sqrt(length))
    sine_part = np.sin(angles) / np.float32(math.sqrt(length))
    forward = np.concatenate(
        [np.concatenate([cosine, -sine_part], 1), np.concatenate([sine_part, cosine], 1)], 0
    )
    backward = np.concatenate(
        [np.concatenate([cosine, sine_part], 1), np.concatenate([-sine_part, cosine], 1)], 0
    )
    pos = np.arange(length)
    order = rate * (pos % (length // rate)) + pos // (length // rate)
    backward = np.concatenate([backward[:, order], backward[:, length + order]], 1)
    return forward.astype(ml_dtypes.bfloat16), backward.astype(ml_dtypes.bfloat16)


def sample_order(length, rate):
    pos = jnp.arange(length, dtype=jnp.int32)
    bins = length // rate
    return rate * (pos % bins) + pos // bins


def detect_kernel(chirp_ref, table_ref, swap_ref, mine_ref, theirs_ref, resp_ref, back_ref, out_ref, pair_ref):
    _, beams, chans_local, width = mine_ref.shape
    trials = resp_ref.shape[0]
    length = width // 2
    bins = length // RATE
    chans = 2 * chans_local
    keep = swap_ref[0] == 0
    mine = mine_ref[0]
    theirs = theirs_ref[0]
    x = jnp.concatenate([jnp.where(keep, mine, theirs), jnp.where(keep, theirs, mine)], axis=1)
    xr = x[:, :, :length].astype(jnp.float32)
    xi = x[:, :, length:].astype(jnp.float32)
    back = back_ref[...]
    pos = lax.broadcasted_iota(jnp.int32, (1, length), 1)
    t = RATE * (pos % bins) + pos // bins
    lane = lax.broadcasted_iota(jnp.int32, (1, 2 * bins), 1)
    rows = beams * chans // 2
    for d in range(trials):
        h = resp_ref[d]
        hr = h[:, :length].astype(jnp.float32)[None]
        hi = h[:, length:].astype(jnp.float32)[None]
        fr = hr * xr - hi * xi
        fi = hr * xi + hi * xr
        joined = jnp.concatenate([fr, fi], -1).reshape(beams * chans, width).astype(jnp.bfloat16)
        series = jnp.dot(joined, back, preferred_element_type=jnp.float32)
        powers = series[:, :length] ** 2 + series[:, length:] ** 2
        powers = jnp.where(t >= chirp_ref[d], powers, jnp.float32(0.0))
        half = powers[:, : length // 2] + powers[:, length // 2 :]
        pair_ref[...] = half + pltpu.roll(half, bins, 1)
        even = pair_ref[pl.ds(0, rows, stride=2), :]
        odd = pair_ref[pl.ds(1, rows, stride=2), :]
        both = jnp.where(lane < bins, even, odd) / RATE
        out_ref[:, d] = both.reshape(beams, chans // 2, 2 * bins).astype(out_ref.dtype)


def detect(table, swap, mine, theirs, responses, chirp_len, backward):
    blocks, beams, chans_local, width = mine.shape
    trials, chans = responses.shape[0], responses.shape[1]
    length = width // 2
    bins = length // RATE
    step = 2 * chans_local
    flops = 2 * trials * beams * chans * width * width
    bytes_accessed = 2 * (2 * mine.size + responses.size + backward.size + trials * beams * chans * bins)
    return pl.pallas_call(
        detect_kernel,
        out_shape=jax.ShapeDtypeStruct((beams, trials, chans // 2, 2 * bins), jnp.bfloat16),
        grid_spec=pltpu.PrefetchScalarGridSpec(
            num_scalar_prefetch=3,
            grid=(chans // step,),
            in_specs=[
                pl.BlockSpec((1, beams, chans_local, width), lambda n, cl, tb, sw: (tb[n], 0, 0, 0)),
                pl.BlockSpec((1, beams, chans_local, width), lambda n, cl, tb, sw: (tb[n], 0, 0, 0)),
                pl.BlockSpec((trials, step, width), lambda n, cl, tb, sw: (0, n, 0)),
                pl.BlockSpec((width, width), lambda n, cl, tb, sw: (0, 0)),
            ],
            out_specs=pl.BlockSpec(
                (beams, trials, step // 2, 2 * bins), lambda n, cl, tb, sw: (0, 0, n, 0)
            ),
            scratch_shapes=[pltpu.VMEM((beams * step, 2 * bins), jnp.float32)],
        ),
        compiler_params=pltpu.CompilerParams(
            dimension_semantics=("arbitrary",), vmem_limit_bytes=48 * 1024 * 1024
        ),
        cost_estimate=pl.CostEstimate(flops=flops, transcendentals=0, bytes_accessed=bytes_accessed),
    )(chirp_len, table, swap, mine, theirs, responses, backward)


def coords(index, z_count):
    return index // (2 * z_count), (index // 2) % z_count, index % 2


def flat(x_lo, z, core, z_count):
    return (x_lo * z_count + z % z_count) * 2 + core


def moves(count, step):
    z_count = count // 4
    pairs = []
    for index in range(count):
        x_lo, z, core = coords(index, z_count)
        pairs.append((index, step(x_lo, z, core, z_count)))
    return pairs


def gather_spectra(own, count):
    z_count = count // 4
    across = moves(count, lambda x, z, c, n: flat(1 - x, z, c, n))
    up = moves(count, lambda x, z, c, n: flat(x, z + 1, c, n))
    down = moves(count, lambda x, z, c, n: flat(x, z - 1, c, n))
    partner = moves(count, lambda x, z, c, n: flat(x, z, 1 - c, n))
    pair = jnp.stack([own, lax.ppermute(own, "dm", across)])
    from_below = [pair]
    from_above = [pair]
    for _ in range(z_count // 2 - 1):
        from_below.append(lax.ppermute(from_below[-1], "dm", up))
        from_above.append(lax.ppermute(from_above[-1], "dm", down))
    far = jnp.stack(
        [lax.ppermute(from_below[-1][0], "dm", up), lax.ppermute(from_above[-1][1], "dm", down)]
    )
    column = jnp.stack(from_above + [far] + from_below[:0:-1])
    column = column.reshape((2 * z_count,) + own.shape)
    return column, lax.ppermute(column, "dm", partner)


def shards(voltages, responses, chirp_len):
    chans_local, beams, _, length = voltages.shape
    trials, chans = responses.shape[0], responses.shape[1]
    count = chans // chans_local
    z_count = count // 4
    forward, backward = (jnp.asarray(table) for table in constant_tables(length, RATE))
    local = jnp.dot(
        voltages.reshape(-1, 2 * length), forward, preferred_element_type=jnp.float32
    ).astype(jnp.bfloat16)
    local = local.reshape(chans_local, beams, 2 * length).transpose(1, 0, 2)
    mine, theirs = gather_spectra(local, count)
    x_me, z_me, c_me = coords(lax.axis_index("dm"), z_count)
    block = jnp.arange(count // 2, dtype=jnp.int32)
    table = ((block % z_count - z_me) % z_count) * 2 + ((block // z_count) ^ x_me)
    swap = jnp.reshape(c_me, (1,)).astype(jnp.int32)
    detected = detect(
        table, swap, mine, theirs, responses.reshape(trials, chans, 2 * length), chirp_len, backward
    )
    moved = lax.all_to_all(detected.transpose(1, 0, 2, 3), "beam", split_axis=1, concat_axis=2, tiled=True)
    return moved.reshape(trials, 1, -1)


def solution(mesh):
    placed = (P(("beam", "dm"), None, None, None), P("dm", "beam", None, None), P("dm"))
    return jax.shard_map(
        shards, mesh=mesh, in_specs=placed, out_specs=P("dm", "beam", None), check_vma=False
    )
```

```python
import functools
import math

import jax
import ml_dtypes
import numpy as np
import jax.numpy as jnp
from jax import lax
from jax.experimental import pallas as pl
from jax.experimental.pallas import tpu as pltpu
from jax.sharding import PartitionSpec as P

RATE = 4
CHAN_BLOCK = 256


def dft_tables(length):
    sample = jnp.arange(length, dtype=jnp.int32)
    phases = sample[:, None] * sample[None, :] % length
    angles = phases.astype(jnp.float32) * (2.0 * math.pi / length)
    cosine = jnp.cos(angles) / math.sqrt(length)
    sine_part = jnp.sin(angles) / math.sqrt(length)
    forward = jnp.concatenate(
        [jnp.concatenate([cosine, -sine_part], 1), jnp.concatenate([sine_part, cosine], 1)], 0
    )
    backward = jnp.concatenate(
        [jnp.concatenate([cosine, sine_part], 1), jnp.concatenate([-sine_part, cosine], 1)], 0
    )
    return (forward.astype(jnp.bfloat16), backward.astype(jnp.bfloat16))


def constant_tables(length, rate):
    sample = np.arange(length, dtype=np.int32)
    phases = sample[:, None] * sample[None, :] % length
    angles = phases.astype(np.float32) * np.float32(2.0 * math.pi / length)
    cosine = np.cos(angles) / np.float32(math.sqrt(length))
    sine_part = np.sin(angles) / np.float32(math.sqrt(length))
    forward = np.concatenate(
        [np.concatenate([cosine, -sine_part], 1), np.concatenate([sine_part, cosine], 1)], 0
    )
    backward = np.concatenate(
        [np.concatenate([cosine, sine_part], 1), np.concatenate([-sine_part, cosine], 1)], 0
    )
    pos = np.arange(length)
    order = rate * (pos % (length // rate)) + pos // (length // rate)
    backward = np.concatenate([backward[:, order], backward[:, length + order]], 1)
    return forward.astype(ml_dtypes.bfloat16), backward.astype(ml_dtypes.bfloat16)


def sample_order(length, rate):
    pos = jnp.arange(length, dtype=jnp.int32)
    bins = length // rate
    return rate * (pos % bins) + pos // bins


def detect_kernel(
    chirp_ref, table_ref, swap_ref, mine0_ref, theirs0_ref, mine1_ref, theirs1_ref, resp_ref, back_ref, out_ref,
    pair_ref,
):
    _, beams, chans_local, width = mine0_ref.shape
    trials = resp_ref.shape[0]
    length = width // 2
    bins = length // RATE
    chans = 4 * chans_local
    keep = swap_ref[0] == 0
    pieces = []
    for mine_ref, theirs_ref in ((mine0_ref, theirs0_ref), (mine1_ref, theirs1_ref)):
        mine = mine_ref[0]
        theirs = theirs_ref[0]
        pieces += [jnp.where(keep, mine, theirs), jnp.where(keep, theirs, mine)]
    x = jnp.concatenate(pieces, axis=1)
    xr = x[:, :, :length].astype(jnp.float32)
    xi = x[:, :, length:].astype(jnp.float32)
    back = back_ref[...]
    pos = lax.broadcasted_iota(jnp.int32, (1, length), 1)
    t = RATE * (pos % bins) + pos // bins
    lane = lax.broadcasted_iota(jnp.int32, (1, 2 * bins), 1)
    rows = beams * chans // 2
    for d in range(trials):
        h = resp_ref[d]
        hr = h[:, :length].astype(jnp.float32)[None]
        hi = h[:, length:].astype(jnp.float32)[None]
        fr = hr * xr - hi * xi
        fi = hr * xi + hi * xr
        joined = jnp.concatenate([fr, fi], -1).reshape(beams * chans, width).astype(jnp.bfloat16)
        series = jnp.dot(joined, back, preferred_element_type=jnp.float32)
        powers = series[:, :length] ** 2 + series[:, length:] ** 2
        powers = jnp.where(t >= chirp_ref[d], powers, jnp.float32(0.0))
        half = powers[:, : length // 2] + powers[:, length // 2 :]
        pair_ref[...] = half + pltpu.roll(half, bins, 1)
        even = pair_ref[pl.ds(0, rows, stride=2), :]
        odd = pair_ref[pl.ds(1, rows, stride=2), :]
        both = jnp.where(lane < bins, even, odd) / RATE
        out_ref[:, d] = both.reshape(beams, chans // 2, 2 * bins).astype(out_ref.dtype)


def detect(table, swap, mine, theirs, responses, chirp_len, backward):
    blocks, beams, chans_local, width = mine.shape
    trials, chans = responses.shape[0], responses.shape[1]
    length = width // 2
    bins = length // RATE
    step = 4 * chans_local
    flops = 2 * trials * beams * chans * width * width
    bytes_accessed = 2 * (2 * mine.size + responses.size + backward.size + trials * beams * chans * bins)
    return pl.pallas_call(
        detect_kernel,
        out_shape=jax.ShapeDtypeStruct((beams, trials, chans // 2, 2 * bins), jnp.bfloat16),
        grid_spec=pltpu.PrefetchScalarGridSpec(
            num_scalar_prefetch=3,
            grid=(chans // step,),
            in_specs=[
                pl.BlockSpec((1, beams, chans_local, width), lambda n, cl, tb, sw: (tb[2 * n], 0, 0, 0)),
                pl.BlockSpec((1, beams, chans_local, width), lambda n, cl, tb, sw: (tb[2 * n], 0, 0, 0)),
                pl.BlockSpec((1, beams, chans_local, width), lambda n, cl, tb, sw: (tb[2 * n + 1], 0, 0, 0)),
                pl.BlockSpec((1, beams, chans_local, width), lambda n, cl, tb, sw: (tb[2 * n + 1], 0, 0, 0)),
                pl.BlockSpec((trials, step, width), lambda n, cl, tb, sw: (0, n, 0)),
                pl.BlockSpec((width, width), lambda n, cl, tb, sw: (0, 0)),
            ],
            out_specs=pl.BlockSpec(
                (beams, trials, step // 2, 2 * bins), lambda n, cl, tb, sw: (0, 0, n, 0)
            ),
            scratch_shapes=[pltpu.VMEM((beams * step, 2 * bins), jnp.float32)],
        ),
        compiler_params=pltpu.CompilerParams(
            dimension_semantics=("arbitrary",), vmem_limit_bytes=48 * 1024 * 1024
        ),
        cost_estimate=pl.CostEstimate(flops=flops, transcendentals=0, bytes_accessed=bytes_accessed),
    )(chirp_len, table, swap, mine, theirs, mine, theirs, responses, backward)


def coords(index, z_count):
    return index // (2 * z_count), (index // 2) % z_count, index % 2


def flat(x_lo, z, core, z_count):
    return (x_lo * z_count + z % z_count) * 2 + core


def moves(count, step):
    z_count = count // 4
    pairs = []
    for index in range(count):
        x_lo, z, core = coords(index, z_count)
        pairs.append((index, step(x_lo, z, core, z_count)))
    return pairs


def gather_spectra(own, count):
    z_count = count // 4
    across = moves(count, lambda x, z, c, n: flat(1 - x, z, c, n))
    up = moves(count, lambda x, z, c, n: flat(x, z + 1, c, n))
    down = moves(count, lambda x, z, c, n: flat(x, z - 1, c, n))
    partner = moves(count, lambda x, z, c, n: flat(x, z, 1 - c, n))
    pair = jnp.stack([own, lax.ppermute(own, "dm", across)])
    from_below = [pair]
    from_above = [pair]
    for _ in range(z_count // 2 - 1):
        from_below.append(lax.ppermute(from_below[-1], "dm", up))
        from_above.append(lax.ppermute(from_above[-1], "dm", down))
    far = jnp.stack(
        [lax.ppermute(from_below[-1][0], "dm", up), lax.ppermute(from_above[-1][1], "dm", down)]
    )
    column = jnp.stack(from_above + [far] + from_below[:0:-1])
    column = column.reshape((2 * z_count,) + own.shape)
    return column, lax.ppermute(column, "dm", partner)


def shards(voltages, responses, chirp_len):
    chans_local, beams, _, length = voltages.shape
    trials, chans = responses.shape[0], responses.shape[1]
    count = chans // chans_local
    z_count = count // 4
    forward, backward = (jnp.asarray(table) for table in constant_tables(length, RATE))
    local = jnp.dot(
        voltages.reshape(-1, 2 * length), forward, preferred_element_type=jnp.float32
    ).astype(jnp.bfloat16)
    local = local.reshape(chans_local, beams, 2 * length).transpose(1, 0, 2)
    mine, theirs = gather_spectra(local, count)
    x_me, z_me, c_me = coords(lax.axis_index("dm"), z_count)
    block = jnp.arange(count // 2, dtype=jnp.int32)
    table = ((block % z_count - z_me) % z_count) * 2 + ((block // z_count) ^ x_me)
    swap = jnp.reshape(c_me, (1,)).astype(jnp.int32)
    detected = detect(
        table, swap, mine, theirs, responses.reshape(trials, chans, 2 * length), chirp_len, backward
    )
    moved = lax.all_to_all(detected.transpose(1, 0, 2, 3), "beam", split_axis=1, concat_axis=2, tiled=True)
    return moved.reshape(trials, 1, -1)


def solution(mesh):
    placed = (P(("beam", "dm"), None, None, None), P("dm", "beam", None, None), P("dm"))
    return jax.shard_map(
        shards, mesh=mesh, in_specs=placed, out_specs=P("dm", "beam", None), check_vma=False
    )
```

```python
import functools
import math

import jax
import ml_dtypes
import numpy as np
import jax.numpy as jnp
from jax import lax
from jax.experimental import pallas as pl
from jax.experimental.pallas import tpu as pltpu
from jax.sharding import PartitionSpec as P

RATE = 4
CHAN_BLOCK = 256
GROUP = 4


def dft_tables(length):
    sample = jnp.arange(length, dtype=jnp.int32)
    phases = sample[:, None] * sample[None, :] % length
    angles = phases.astype(jnp.float32) * (2.0 * math.pi / length)
    cosine = jnp.cos(angles) / math.sqrt(length)
    sine_part = jnp.sin(angles) / math.sqrt(length)
    forward = jnp.concatenate(
        [jnp.concatenate([cosine, -sine_part], 1), jnp.concatenate([sine_part, cosine], 1)], 0
    )
    backward = jnp.concatenate(
        [jnp.concatenate([cosine, sine_part], 1), jnp.concatenate([-sine_part, cosine], 1)], 0
    )
    return (forward.astype(jnp.bfloat16), backward.astype(jnp.bfloat16))


def constant_tables(length, rate):
    sample = np.arange(length, dtype=np.int32)
    phases = sample[:, None] * sample[None, :] % length
    angles = phases.astype(np.float32) * np.float32(2.0 * math.pi / length)
    cosine = np.cos(angles) / np.float32(math.sqrt(length))
    sine_part = np.sin(angles) / np.float32(math.sqrt(length))
    forward = np.concatenate(
        [np.concatenate([cosine, -sine_part], 1), np.concatenate([sine_part, cosine], 1)], 0
    )
    backward = np.concatenate(
        [np.concatenate([cosine, sine_part], 1), np.concatenate([-sine_part, cosine], 1)], 0
    )
    pos = np.arange(length)
    order = rate * (pos % (length // rate)) + pos // (length // rate)
    backward = np.concatenate([backward[:, order], backward[:, length + order]], 1)
    return forward.astype(ml_dtypes.bfloat16), backward.astype(ml_dtypes.bfloat16)


def sample_order(length, rate):
    pos = jnp.arange(length, dtype=jnp.int32)
    bins = length // rate
    return rate * (pos % bins) + pos // bins


def detect_kernel(chirp_ref, table_ref, swap_ref, *refs):
    spec_refs = refs[: 2 * GROUP]
    resp_ref, back_ref, out_ref, pair_ref = refs[2 * GROUP :]
    _, beams, chans_local, width = spec_refs[0].shape
    trials = resp_ref.shape[0]
    length = width // 2
    bins = length // RATE
    chans = 2 * GROUP * chans_local
    keep = swap_ref[0] == 0
    pieces = []
    for g in range(GROUP):
        mine = spec_refs[2 * g][0]
        theirs = spec_refs[2 * g + 1][0]
        pieces += [jnp.where(keep, mine, theirs), jnp.where(keep, theirs, mine)]
    x = jnp.concatenate(pieces, axis=1)
    xr = x[:, :, :length].astype(jnp.float32)
    xi = x[:, :, length:].astype(jnp.float32)
    back = back_ref[...]
    pos = lax.broadcasted_iota(jnp.int32, (1, length), 1)
    t = RATE * (pos % bins) + pos // bins
    lane = lax.broadcasted_iota(jnp.int32, (1, 2 * bins), 1)
    rows = beams * chans // 2
    for d in range(trials):
        h = resp_ref[d]
        hr = h[:, :length].astype(jnp.float32)[None]
        hi = h[:, length:].astype(jnp.float32)[None]
        fr = hr * xr - hi * xi
        fi = hr * xi + hi * xr
        joined = jnp.concatenate([fr, fi], -1).reshape(beams * chans, width).astype(jnp.bfloat16)
        series = jnp.dot(joined, back, preferred_element_type=jnp.float32)
        powers = series[:, :length] ** 2 + series[:, length:] ** 2
        powers = jnp.where(t >= chirp_ref[d], powers, jnp.float32(0.0))
        half = powers[:, : length // 2] + powers[:, length // 2 :]
        pair_ref[...] = half + pltpu.roll(half, bins, 1)
        even = pair_ref[pl.ds(0, rows, stride=2), :]
        odd = pair_ref[pl.ds(1, rows, stride=2), :]
        both = jnp.where(lane < bins, even, odd) / RATE
        out_ref[:, d] = both.reshape(beams, chans // 2, 2 * bins).astype(out_ref.dtype)


def detect(table, swap, mine, theirs, responses, chirp_len, backward):
    blocks, beams, chans_local, width = mine.shape
    trials, chans = responses.shape[0], responses.shape[1]
    length = width // 2
    bins = length // RATE
    step = 2 * GROUP * chans_local
    flops = 2 * trials * beams * chans * width * width
    bytes_accessed = 2 * (2 * mine.size + responses.size + backward.size + trials * beams * chans * bins)
    spec_specs = []
    for g in range(GROUP):
        spec = pl.BlockSpec(
            (1, beams, chans_local, width), lambda n, cl, tb, sw, g=g: (tb[GROUP * n + g], 0, 0, 0)
        )
        spec_specs += [spec, spec]
    return pl.pallas_call(
        detect_kernel,
        out_shape=jax.ShapeDtypeStruct((beams, trials, chans // 2, 2 * bins), jnp.bfloat16),
        grid_spec=pltpu.PrefetchScalarGridSpec(
            num_scalar_prefetch=3,
            grid=(chans // step,),
            in_specs=spec_specs + [
                pl.BlockSpec((trials, step, width), lambda n, cl, tb, sw: (0, n, 0)),
                pl.BlockSpec((width, width), lambda n, cl, tb, sw: (0, 0)),
            ],
            out_specs=pl.BlockSpec(
                (beams, trials, step // 2, 2 * bins), lambda n, cl, tb, sw: (0, 0, n, 0)
            ),
            scratch_shapes=[pltpu.VMEM((beams * step, 2 * bins), jnp.float32)],
        ),
        compiler_params=pltpu.CompilerParams(
            dimension_semantics=("arbitrary",), vmem_limit_bytes=48 * 1024 * 1024
        ),
        cost_estimate=pl.CostEstimate(flops=flops, transcendentals=0, bytes_accessed=bytes_accessed),
    )(chirp_len, table, swap, *([mine, theirs] * GROUP), responses, backward)


def coords(index, z_count):
    return index // (2 * z_count), (index // 2) % z_count, index % 2


def flat(x_lo, z, core, z_count):
    return (x_lo * z_count + z % z_count) * 2 + core


def moves(count, step):
    z_count = count // 4
    pairs = []
    for index in range(count):
        x_lo, z, core = coords(index, z_count)
        pairs.append((index, step(x_lo, z, core, z_count)))
    return pairs


def gather_spectra(own, count):
    z_count = count // 4
    across = moves(count, lambda x, z, c, n: flat(1 - x, z, c, n))
    up = moves(count, lambda x, z, c, n: flat(x, z + 1, c, n))
    down = moves(count, lambda x, z, c, n: flat(x, z - 1, c, n))
    partner = moves(count, lambda x, z, c, n: flat(x, z, 1 - c, n))
    pair = jnp.stack([own, lax.ppermute(own, "dm", across)])
    from_below = [pair]
    from_above = [pair]
    for _ in range(z_count // 2 - 1):
        from_below.append(lax.ppermute(from_below[-1], "dm", up))
        from_above.append(lax.ppermute(from_above[-1], "dm", down))
    far = jnp.stack(
        [lax.ppermute(from_below[-1][0], "dm", up), lax.ppermute(from_above[-1][1], "dm", down)]
    )
    column = jnp.stack(from_above + [far] + from_below[:0:-1])
    column = column.reshape((2 * z_count,) + own.shape)
    return column, lax.ppermute(column, "dm", partner)


def shards(voltages, responses, chirp_len):
    chans_local, beams, _, length = voltages.shape
    trials, chans = responses.shape[0], responses.shape[1]
    count = chans // chans_local
    z_count = count // 4
    forward, backward = (jnp.asarray(table) for table in constant_tables(length, RATE))
    local = jnp.dot(
        voltages.reshape(-1, 2 * length), forward, preferred_element_type=jnp.float32
    ).astype(jnp.bfloat16)
    local = local.reshape(chans_local, beams, 2 * length).transpose(1, 0, 2)
    mine, theirs = gather_spectra(local, count)
    x_me, z_me, c_me = coords(lax.axis_index("dm"), z_count)
    block = jnp.arange(count // 2, dtype=jnp.int32)
    table = ((block % z_count - z_me) % z_count) * 2 + ((block // z_count) ^ x_me)
    swap = jnp.reshape(c_me, (1,)).astype(jnp.int32)
    detected = detect(
        table, swap, mine, theirs, responses.reshape(trials, chans, 2 * length), chirp_len, backward
    )
    moved = lax.all_to_all(detected.transpose(1, 0, 2, 3), "beam", split_axis=1, concat_axis=2, tiled=True)
    return moved.reshape(trials, 1, -1)


def solution(mesh):
    placed = (P(("beam", "dm"), None, None, None), P("dm", "beam", None, None), P("dm"))
    return jax.shard_map(
        shards, mesh=mesh, in_specs=placed, out_specs=P("dm", "beam", None), check_vma=False
    )
```

```python
import functools
import math

import jax
import ml_dtypes
import numpy as np
import jax.numpy as jnp
from jax import lax
from jax.experimental import pallas as pl
from jax.experimental.pallas import tpu as pltpu
from jax.sharding import PartitionSpec as P

RATE = 4
CHAN_BLOCK = 256
GROUP = 4


def dft_tables(length):
    sample = jnp.arange(length, dtype=jnp.int32)
    phases = sample[:, None] * sample[None, :] % length
    angles = phases.astype(jnp.float32) * (2.0 * math.pi / length)
    cosine = jnp.cos(angles) / math.sqrt(length)
    sine_part = jnp.sin(angles) / math.sqrt(length)
    forward = jnp.concatenate(
        [jnp.concatenate([cosine, -sine_part], 1), jnp.concatenate([sine_part, cosine], 1)], 0
    )
    backward = jnp.concatenate(
        [jnp.concatenate([cosine, sine_part], 1), jnp.concatenate([-sine_part, cosine], 1)], 0
    )
    return (forward.astype(jnp.bfloat16), backward.astype(jnp.bfloat16))


def constant_tables(length, rate):
    sample = np.arange(length, dtype=np.int32)
    phases = sample[:, None] * sample[None, :] % length
    angles = phases.astype(np.float32) * np.float32(2.0 * math.pi / length)
    cosine = np.cos(angles) / np.float32(math.sqrt(length))
    sine_part = np.sin(angles) / np.float32(math.sqrt(length))
    forward = np.concatenate(
        [np.concatenate([cosine, -sine_part], 1), np.concatenate([sine_part, cosine], 1)], 0
    )
    backward = np.concatenate(
        [np.concatenate([cosine, sine_part], 1), np.concatenate([-sine_part, cosine], 1)], 0
    )
    pos = np.arange(length)
    order = rate * (pos % (length // rate)) + pos // (length // rate)
    backward = np.concatenate([backward[:, order], backward[:, length + order]], 1)
    return forward.astype(ml_dtypes.bfloat16), backward.astype(ml_dtypes.bfloat16)


def sample_order(length, rate):
    pos = jnp.arange(length, dtype=jnp.int32)
    bins = length // rate
    return rate * (pos % bins) + pos // bins


def detect_kernel(chirp_ref, table_ref, swap_ref, *refs):
    spec_refs = refs[: 2 * GROUP]
    resp_ref, back_ref, out_ref, pair_ref = refs[2 * GROUP :]
    _, beams, chans_local, width = spec_refs[0].shape
    trials = resp_ref.shape[0]
    length = width // 2
    bins = length // RATE
    chans = 2 * GROUP * chans_local
    keep = swap_ref[0] == 0
    pieces = []
    for g in range(GROUP):
        mine = spec_refs[2 * g][0]
        theirs = spec_refs[2 * g + 1][0]
        pieces += [jnp.where(keep, mine, theirs), jnp.where(keep, theirs, mine)]
    x = jnp.concatenate(pieces, axis=1)
    xr = x[:, :, :length].astype(jnp.float32)
    xi = x[:, :, length:].astype(jnp.float32)
    back = back_ref[...]
    pos = lax.broadcasted_iota(jnp.int32, (1, length), 1)
    t = RATE * (pos % bins) + pos // bins
    lane = lax.broadcasted_iota(jnp.int32, (1, 2 * bins), 1)
    rows = beams * chans // 2
    for d in range(trials):
        h = resp_ref[d]
        hr = h[:, :length].astype(jnp.float32)[None]
        hi = h[:, length:].astype(jnp.float32)[None]
        fr = hr * xr - hi * xi
        fi = hr * xi + hi * xr
        joined = jnp.concatenate([fr, fi], -1).reshape(beams * chans, width).astype(jnp.bfloat16)
        series = jnp.dot(joined, back, preferred_element_type=jnp.float32)
        powers = series[:, :length] ** 2 + series[:, length:] ** 2
        powers = jnp.where(t >= chirp_ref[d], powers, jnp.float32(0.0))
        half = powers[:, : length // 2] + powers[:, length // 2 :]
        pair_ref[...] = half + pltpu.roll(half, bins, 1)
        even = pair_ref[pl.ds(0, rows, stride=2), :]
        odd = pair_ref[pl.ds(1, rows, stride=2), :]
        both = jnp.where(lane < bins, even, odd) / RATE
        out_ref[:, d] = both.reshape(beams, chans // 2, 2 * bins).astype(out_ref.dtype)


def detect(table, swap, mine, theirs, responses, chirp_len, backward):
    blocks, beams, chans_local, width = mine.shape
    trials, chans = responses.shape[0], responses.shape[1]
    length = width // 2
    bins = length // RATE
    step = 2 * GROUP * chans_local
    flops = 2 * trials * beams * chans * width * width
    bytes_accessed = 2 * (2 * mine.size + responses.size + backward.size + trials * beams * chans * bins)
    spec_specs = []
    for g in range(GROUP):
        spec = pl.BlockSpec(
            (1, beams, chans_local, width), lambda n, cl, tb, sw, g=g: (tb[GROUP * n + g], 0, 0, 0)
        )
        spec_specs += [spec, spec]
    return pl.pallas_call(
        detect_kernel,
        out_shape=jax.ShapeDtypeStruct((beams, trials, chans // 2, 2 * bins), jnp.bfloat16),
        grid_spec=pltpu.PrefetchScalarGridSpec(
            num_scalar_prefetch=3,
            grid=(chans // step,),
            in_specs=spec_specs + [
                pl.BlockSpec((trials, step, width), lambda n, cl, tb, sw: (0, n, 0)),
                pl.BlockSpec((width, width), lambda n, cl, tb, sw: (0, 0)),
            ],
            out_specs=pl.BlockSpec(
                (beams, trials, step // 2, 2 * bins), lambda n, cl, tb, sw: (0, 0, n, 0)
            ),
            scratch_shapes=[pltpu.VMEM((beams * step, 2 * bins), jnp.float32)],
        ),
        compiler_params=pltpu.CompilerParams(
            dimension_semantics=("arbitrary",), vmem_limit_bytes=48 * 1024 * 1024
        ),
        cost_estimate=pl.CostEstimate(flops=flops, transcendentals=0, bytes_accessed=bytes_accessed),
    )(chirp_len, table, swap, *([mine, theirs] * GROUP), responses, backward)


def coords(index, z_count):
    return index // (2 * z_count), (index // 2) % z_count, index % 2


def flat(x_lo, z, core, z_count):
    return (x_lo * z_count + z % z_count) * 2 + core


def moves(count, step):
    z_count = count // 4
    pairs = []
    for index in range(count):
        x_lo, z, core = coords(index, z_count)
        pairs.append((index, step(x_lo, z, core, z_count)))
    return pairs


def gather_spectra(own, count, carried):
    z_count = count // 4
    across = moves(count, lambda x, z, c, n: flat(1 - x, z, c, n))
    up = moves(count, lambda x, z, c, n: flat(x, z + 1, c, n))
    down = moves(count, lambda x, z, c, n: flat(x, z - 1, c, n))
    partner = moves(count, lambda x, z, c, n: flat(x, z, 1 - c, n))
    pair = jnp.stack([own, lax.ppermute(own, "dm", across)])
    from_below = [pair]
    from_above = [pair]
    for k in range(z_count // 2 - 1):
        from_below.append(lax.ppermute(from_below[-1], "dm", up))
        from_above.append(lax.ppermute(from_above[-1], "dm", down))
        if k == 0:
            from_below[-1], from_above[-1], carried = lax.optimization_barrier(
                (from_below[-1], from_above[-1], carried)
            )
    far = jnp.stack(
        [lax.ppermute(from_below[-1][0], "dm", up), lax.ppermute(from_above[-1][1], "dm", down)]
    )
    column = jnp.stack(from_above + [far] + from_below[:0:-1])
    column = column.reshape((2 * z_count,) + own.shape)
    return column, lax.ppermute(column, "dm", partner), carried


def shards(voltages, responses, chirp_len):
    chans_local, beams, _, length = voltages.shape
    trials, chans = responses.shape[0], responses.shape[1]
    count = chans // chans_local
    z_count = count // 4
    forward, backward = (jnp.asarray(table) for table in constant_tables(length, RATE))
    local = jnp.dot(
        voltages.reshape(-1, 2 * length), forward, preferred_element_type=jnp.float32
    ).astype(jnp.bfloat16)
    local = local.reshape(chans_local, beams, 2 * length).transpose(1, 0, 2)
    resp = responses.reshape(trials, chans, 2 * length)
    mine, theirs, resp = gather_spectra(local, count, resp)
    x_me, z_me, c_me = coords(lax.axis_index("dm"), z_count)
    block = jnp.arange(count // 2, dtype=jnp.int32)
    table = ((block % z_count - z_me) % z_count) * 2 + ((block // z_count) ^ x_me)
    swap = jnp.reshape(c_me, (1,)).astype(jnp.int32)
    detected = detect(
        table, swap, mine, theirs, resp, chirp_len, backward
    )
    moved = lax.all_to_all(detected.transpose(1, 0, 2, 3), "beam", split_axis=1, concat_axis=2, tiled=True)
    return moved.reshape(trials, 1, -1)


def solution(mesh):
    placed = (P(("beam", "dm"), None, None, None), P("dm", "beam", None, None), P("dm"))
    return jax.shard_map(
        shards, mesh=mesh, in_specs=placed, out_specs=P("dm", "beam", None), check_vma=False
    )
```

```python
import functools
import math

import jax
import ml_dtypes
import numpy as np
import jax.numpy as jnp
from jax import lax
from jax.experimental import pallas as pl
from jax.experimental.pallas import tpu as pltpu
from jax.sharding import PartitionSpec as P

RATE = 4
CHAN_BLOCK = 256
GROUP = 4


def dft_tables(length):
    sample = jnp.arange(length, dtype=jnp.int32)
    phases = sample[:, None] * sample[None, :] % length
    angles = phases.astype(jnp.float32) * (2.0 * math.pi / length)
    cosine = jnp.cos(angles) / math.sqrt(length)
    sine_part = jnp.sin(angles) / math.sqrt(length)
    forward = jnp.concatenate(
        [jnp.concatenate([cosine, -sine_part], 1), jnp.concatenate([sine_part, cosine], 1)], 0
    )
    backward = jnp.concatenate(
        [jnp.concatenate([cosine, sine_part], 1), jnp.concatenate([-sine_part, cosine], 1)], 0
    )
    return (forward.astype(jnp.bfloat16), backward.astype(jnp.bfloat16))


def constant_tables(length, rate):
    sample = np.arange(length, dtype=np.int32)
    phases = sample[:, None] * sample[None, :] % length
    angles = phases.astype(np.float32) * np.float32(2.0 * math.pi / length)
    cosine = np.cos(angles) / np.float32(math.sqrt(length))
    sine_part = np.sin(angles) / np.float32(math.sqrt(length))
    forward = np.concatenate(
        [np.concatenate([cosine, -sine_part], 1), np.concatenate([sine_part, cosine], 1)], 0
    )
    backward = np.concatenate(
        [np.concatenate([cosine, sine_part], 1), np.concatenate([-sine_part, cosine], 1)], 0
    )
    pos = np.arange(length)
    order = rate * (pos % (length // rate)) + pos // (length // rate)
    backward = np.concatenate([backward[:, order], backward[:, length + order]], 1)
    return forward.astype(ml_dtypes.bfloat16), backward.astype(ml_dtypes.bfloat16)


def sample_order(length, rate):
    pos = jnp.arange(length, dtype=jnp.int32)
    bins = length // rate
    return rate * (pos % bins) + pos // bins


def detect_kernel(chirp_ref, table_ref, early_ref, late_ref, flag_ref, swap_ref, *refs):
    spec_refs = refs[: 3 * GROUP]
    resp_ref, back_ref, out_ref, pair_ref = refs[3 * GROUP :]
    _, beams, chans_local, width = spec_refs[0].shape
    trials = resp_ref.shape[0]
    length = width // 2
    bins = length // RATE
    chans = 2 * GROUP * chans_local
    keep = swap_ref[0] == 0
    pieces = []
    for g in range(GROUP):
        mine = spec_refs[3 * g][0]
        late = flag_ref[GROUP * pl.program_id(0) + g] != 0
        theirs = jnp.where(late, spec_refs[3 * g + 2][0], spec_refs[3 * g + 1][0])
        pieces += [jnp.where(keep, mine, theirs), jnp.where(keep, theirs, mine)]
    x = jnp.concatenate(pieces, axis=1)
    xr = x[:, :, :length].astype(jnp.float32)
    xi = x[:, :, length:].astype(jnp.float32)
    back = back_ref[...]
    pos = lax.broadcasted_iota(jnp.int32, (1, length), 1)
    t = RATE * (pos % bins) + pos // bins
    lane = lax.broadcasted_iota(jnp.int32, (1, 2 * bins), 1)
    rows = beams * chans // 2
    for d in range(trials):
        h = resp_ref[d]
        hr = h[:, :length].astype(jnp.float32)[None]
        hi = h[:, length:].astype(jnp.float32)[None]
        fr = hr * xr - hi * xi
        fi = hr * xi + hi * xr
        joined = jnp.concatenate([fr, fi], -1).reshape(beams * chans, width).astype(jnp.bfloat16)
        series = jnp.dot(joined, back, preferred_element_type=jnp.float32)
        powers = series[:, :length] ** 2 + series[:, length:] ** 2
        powers = jnp.where(t >= chirp_ref[d], powers, jnp.float32(0.0))
        half = powers[:, : length // 2] + powers[:, length // 2 :]
        pair_ref[...] = half + pltpu.roll(half, bins, 1)
        even = pair_ref[pl.ds(0, rows, stride=2), :]
        odd = pair_ref[pl.ds(1, rows, stride=2), :]
        both = jnp.where(lane < bins, even, odd) / RATE
        out_ref[:, d] = both.reshape(beams, chans // 2, 2 * bins).astype(out_ref.dtype)


def detect(tables, swap, mine, theirs_early, theirs_late, responses, chirp_len, backward):
    blocks, beams, chans_local, width = mine.shape
    trials, chans = responses.shape[0], responses.shape[1]
    length = width // 2
    bins = length // RATE
    step = 2 * GROUP * chans_local
    flops = 2 * trials * beams * chans * width * width
    bytes_accessed = 2 * (2 * mine.size + responses.size + backward.size + trials * beams * chans * bins)
    spec_specs = []
    for g in range(GROUP):
        for which in range(3):
            spec_specs.append(
                pl.BlockSpec(
                    (1, beams, chans_local, width),
                    lambda n, cl, tb, te, tl, fl, sw, g=g, which=which: (
                        (tb, te, tl)[which][GROUP * n + g], 0, 0, 0
                    ),
                )
            )
    return pl.pallas_call(
        detect_kernel,
        out_shape=jax.ShapeDtypeStruct((beams, trials, chans // 2, 2 * bins), jnp.bfloat16),
        grid_spec=pltpu.PrefetchScalarGridSpec(
            num_scalar_prefetch=6,
            grid=(chans // step,),
            in_specs=spec_specs + [
                pl.BlockSpec((trials, step, width), lambda n, cl, tb, te, tl, fl, sw: (0, n, 0)),
                pl.BlockSpec((width, width), lambda n, cl, tb, te, tl, fl, sw: (0, 0)),
            ],
            out_specs=pl.BlockSpec(
                (beams, trials, step // 2, 2 * bins), lambda n, cl, tb, te, tl, fl, sw: (0, 0, n, 0)
            ),
            scratch_shapes=[pltpu.VMEM((beams * step, 2 * bins), jnp.float32)],
        ),
        compiler_params=pltpu.CompilerParams(
            dimension_semantics=("arbitrary",), vmem_limit_bytes=48 * 1024 * 1024
        ),
        cost_estimate=pl.CostEstimate(flops=flops, transcendentals=0, bytes_accessed=bytes_accessed),
    )(chirp_len, *tables, swap, *([mine, theirs_early, theirs_late] * GROUP), responses, backward)


def coords(index, z_count):
    return index // (2 * z_count), (index // 2) % z_count, index % 2


def flat(x_lo, z, core, z_count):
    return (x_lo * z_count + z % z_count) * 2 + core


def moves(count, step):
    z_count = count // 4
    pairs = []
    for index in range(count):
        x_lo, z, core = coords(index, z_count)
        pairs.append((index, step(x_lo, z, core, z_count)))
    return pairs


def gather_spectra(own, count, carried):
    z_count = count // 4
    across = moves(count, lambda x, z, c, n: flat(1 - x, z, c, n))
    up = moves(count, lambda x, z, c, n: flat(x, z + 1, c, n))
    down = moves(count, lambda x, z, c, n: flat(x, z - 1, c, n))
    partner = moves(count, lambda x, z, c, n: flat(x, z, 1 - c, n))
    pair = jnp.stack([own, lax.ppermute(own, "dm", across)])
    from_below = [pair]
    from_above = [pair]
    for k in range(z_count // 2 - 1):
        from_below.append(lax.ppermute(from_below[-1], "dm", up))
        from_above.append(lax.ppermute(from_above[-1], "dm", down))
        if k == 0:
            from_below[-1], from_above[-1], carried = lax.optimization_barrier(
                (from_below[-1], from_above[-1], carried)
            )
    far = jnp.stack(
        [lax.ppermute(from_below[-1][0], "dm", up), lax.ppermute(from_above[-1][1], "dm", down)]
    )
    near = z_count // 4 + 1
    early = jnp.stack(from_above[:near] + from_below[near - 1 : 0 : -1])
    early = early.reshape((-1,) + own.shape)
    theirs_early = lax.ppermute(early, "dm", partner)
    column = jnp.stack(from_above + [far] + from_below[:0:-1])
    column = column.reshape((2 * z_count,) + own.shape)
    late = column[2 * near : 2 * (z_count - near + 1)]
    return column, theirs_early, lax.ppermute(late, "dm", partner), carried


def shards(voltages, responses, chirp_len):
    chans_local, beams, _, length = voltages.shape
    trials, chans = responses.shape[0], responses.shape[1]
    count = chans // chans_local
    z_count = count // 4
    forward, backward = (jnp.asarray(table) for table in constant_tables(length, RATE))
    local = jnp.dot(
        voltages.reshape(-1, 2 * length), forward, preferred_element_type=jnp.float32
    ).astype(jnp.bfloat16)
    local = local.reshape(chans_local, beams, 2 * length).transpose(1, 0, 2)
    resp = responses.reshape(trials, chans, 2 * length)
    mine, theirs_early, theirs_late, resp = gather_spectra(local, count, resp)
    x_me, z_me, c_me = coords(lax.axis_index("dm"), z_count)
    block = jnp.arange(count // 2, dtype=jnp.int32)
    table = ((block % z_count - z_me) % z_count) * 2 + ((block // z_count) ^ x_me)
    swap = jnp.reshape(c_me, (1,)).astype(jnp.int32)
    near = z_count // 4 + 1
    z_rel, x_rel = table // 2, table % 2
    is_late = (z_rel >= near) & (z_rel <= z_count - near)
    early_index = jnp.where(z_rel < near, z_rel, z_rel - (z_count - 2 * near + 1))
    tables = (
        table,
        jnp.where(is_late, 0, early_index * 2 + x_rel),
        jnp.where(is_late, (z_rel - near) * 2 + x_rel, 0),
        is_late.astype(jnp.int32),
    )
    detected = detect(tables, swap, mine, theirs_early, theirs_late, resp, chirp_len, backward)
    moved = lax.all_to_all(detected.transpose(1, 0, 2, 3), "beam", split_axis=1, concat_axis=2, tiled=True)
    return moved.reshape(trials, 1, -1)


def solution(mesh):
    placed = (P(("beam", "dm"), None, None, None), P("dm", "beam", None, None), P("dm"))
    return jax.shard_map(
        shards, mesh=mesh, in_specs=placed, out_specs=P("dm", "beam", None), check_vma=False
    )
```

```python
import functools
import math

import jax
import ml_dtypes
import numpy as np
import jax.numpy as jnp
from jax import lax
from jax.experimental import pallas as pl
from jax.experimental.pallas import tpu as pltpu
from jax.sharding import PartitionSpec as P

RATE = 4
CHAN_BLOCK = 256
GROUP = 4


def dft_tables(length):
    sample = jnp.arange(length, dtype=jnp.int32)
    phases = sample[:, None] * sample[None, :] % length
    angles = phases.astype(jnp.float32) * (2.0 * math.pi / length)
    cosine = jnp.cos(angles) / math.sqrt(length)
    sine_part = jnp.sin(angles) / math.sqrt(length)
    forward = jnp.concatenate(
        [jnp.concatenate([cosine, -sine_part], 1), jnp.concatenate([sine_part, cosine], 1)], 0
    )
    backward = jnp.concatenate(
        [jnp.concatenate([cosine, sine_part], 1), jnp.concatenate([-sine_part, cosine], 1)], 0
    )
    return (forward.astype(jnp.bfloat16), backward.astype(jnp.bfloat16))


def constant_tables(length, rate):
    sample = np.arange(length, dtype=np.int32)
    phases = sample[:, None] * sample[None, :] % length
    angles = phases.astype(np.float32) * np.float32(2.0 * math.pi / length)
    cosine = np.cos(angles) / np.float32(math.sqrt(length))
    sine_part = np.sin(angles) / np.float32(math.sqrt(length))
    forward = np.concatenate(
        [np.concatenate([cosine, -sine_part], 1), np.concatenate([sine_part, cosine], 1)], 0
    )
    backward = np.concatenate(
        [np.concatenate([cosine, sine_part], 1), np.concatenate([-sine_part, cosine], 1)], 0
    )
    pos = np.arange(length)
    order = rate * (pos % (length // rate)) + pos // (length // rate)
    backward = np.concatenate([backward[:, order], backward[:, length + order]], 1)
    return forward.astype(ml_dtypes.bfloat16), backward.astype(ml_dtypes.bfloat16)


def sample_order(length, rate):
    pos = jnp.arange(length, dtype=jnp.int32)
    bins = length // rate
    return rate * (pos % bins) + pos // bins


def detect_kernel(chirp_ref, table_ref, early_ref, late_ref, flag_ref, swap_ref, *refs):
    spec_refs = refs[: 3 * GROUP]
    resp_ref, back_ref, out_ref, pair_ref = refs[3 * GROUP :]
    _, beams, chans_local, width = spec_refs[0].shape
    trials = resp_ref.shape[0]
    length = width // 2
    bins = length // RATE
    chans = 2 * GROUP * chans_local
    keep = swap_ref[0] == 0
    pieces = []
    for g in range(GROUP):
        mine = spec_refs[3 * g][0]
        late = flag_ref[GROUP * pl.program_id(0) + g] != 0
        theirs = jnp.where(late, spec_refs[3 * g + 2][0], spec_refs[3 * g + 1][0])
        pieces += [jnp.where(keep, mine, theirs), jnp.where(keep, theirs, mine)]
    x = jnp.concatenate(pieces, axis=1)
    xr = x[:, :, :length].astype(jnp.float32)
    xi = x[:, :, length:].astype(jnp.float32)
    back = back_ref[...]
    pos = lax.broadcasted_iota(jnp.int32, (1, length), 1)
    t = RATE * (pos % bins) + pos // bins
    lane = lax.broadcasted_iota(jnp.int32, (1, 2 * bins), 1)
    rows = beams * chans // 2
    for d in range(trials):
        h = resp_ref[d]
        hr = h[:, :length].astype(jnp.float32)[None]
        hi = h[:, length:].astype(jnp.float32)[None]
        fr = hr * xr - hi * xi
        fi = hr * xi + hi * xr
        joined = jnp.concatenate([fr, fi], -1).reshape(beams * chans, width).astype(jnp.bfloat16)
        series = jnp.dot(joined, back, preferred_element_type=jnp.float32)
        powers = series[:, :length] ** 2 + series[:, length:] ** 2
        powers = jnp.where(t >= chirp_ref[d], powers, jnp.float32(0.0))
        half = powers[:, : length // 2] + powers[:, length // 2 :]
        pair_ref[...] = half + pltpu.roll(half, bins, 1)
        even = pair_ref[pl.ds(0, rows, stride=2), :]
        odd = pair_ref[pl.ds(1, rows, stride=2), :]
        both = jnp.where(lane < bins, even, odd) / RATE
        out_ref[:, d] = both.reshape(beams, chans // 2, 2 * bins).astype(out_ref.dtype)


def detect(tables, swap, mine, theirs_early, theirs_late, responses, chirp_len, backward):
    blocks, beams, chans_local, width = mine.shape
    trials, chans = responses.shape[0], responses.shape[1]
    length = width // 2
    bins = length // RATE
    step = 2 * GROUP * chans_local
    flops = 2 * trials * beams * chans * width * width
    bytes_accessed = 2 * (2 * mine.size + responses.size + backward.size + trials * beams * chans * bins)
    spec_specs = []
    for g in range(GROUP):
        for which in range(3):
            spec_specs.append(
                pl.BlockSpec(
                    (1, beams, chans_local, width),
                    lambda n, cl, tb, te, tl, fl, sw, g=g, which=which: (
                        (tb, te, tl)[which][GROUP * n + g], 0, 0, 0
                    ),
                )
            )
    return pl.pallas_call(
        detect_kernel,
        out_shape=jax.ShapeDtypeStruct((beams, trials, chans // 2, 2 * bins), jnp.bfloat16),
        grid_spec=pltpu.PrefetchScalarGridSpec(
            num_scalar_prefetch=6,
            grid=(chans // step,),
            in_specs=spec_specs + [
                pl.BlockSpec((trials, step, width), lambda n, cl, tb, te, tl, fl, sw: (0, n, 0)),
                pl.BlockSpec((width, width), lambda n, cl, tb, te, tl, fl, sw: (0, 0)),
            ],
            out_specs=pl.BlockSpec(
                (beams, trials, step // 2, 2 * bins), lambda n, cl, tb, te, tl, fl, sw: (0, 0, n, 0)
            ),
            scratch_shapes=[pltpu.VMEM((beams * step, 2 * bins), jnp.float32)],
        ),
        compiler_params=pltpu.CompilerParams(
            dimension_semantics=("arbitrary",), vmem_limit_bytes=48 * 1024 * 1024
        ),
        cost_estimate=pl.CostEstimate(flops=flops, transcendentals=0, bytes_accessed=bytes_accessed),
    )(chirp_len, *tables, swap, *([mine, theirs_early, theirs_late] * GROUP), responses, backward)


def coords(index, z_count):
    return index // (2 * z_count), (index // 2) % z_count, index % 2


def flat(x_lo, z, core, z_count):
    return (x_lo * z_count + z % z_count) * 2 + core


def moves(count, step):
    z_count = count // 4
    pairs = []
    for index in range(count):
        x_lo, z, core = coords(index, z_count)
        pairs.append((index, step(x_lo, z, core, z_count)))
    return pairs


def gather_spectra(own, count, carried):
    z_count = count // 4
    across = moves(count, lambda x, z, c, n: flat(1 - x, z, c, n))
    up = moves(count, lambda x, z, c, n: flat(x, z + 1, c, n))
    down = moves(count, lambda x, z, c, n: flat(x, z - 1, c, n))
    partner = moves(count, lambda x, z, c, n: flat(x, z, 1 - c, n))
    pair = jnp.stack([own, lax.ppermute(own, "dm", across)])
    from_below = [pair]
    from_above = [pair]
    for k in range(z_count // 2 - 1):
        from_below.append(lax.ppermute(from_below[-1], "dm", up))
        from_above.append(lax.ppermute(from_above[-1], "dm", down))
        if k == 0:
            from_below[-1], from_above[-1], carried = lax.optimization_barrier(
                (from_below[-1], from_above[-1], carried)
            )
    near = z_count // 4 + 1
    early = jnp.stack(from_above[:near] + from_below[near - 1 : 0 : -1])
    early = early.reshape((-1,) + own.shape)
    theirs_early = lax.ppermute(early, "dm", partner)
    from_below[-1], from_above[-1], theirs_early = lax.optimization_barrier(
        (from_below[-1], from_above[-1], theirs_early)
    )
    far = jnp.stack(
        [lax.ppermute(from_below[-1][0], "dm", up), lax.ppermute(from_above[-1][1], "dm", down)]
    )
    column = jnp.stack(from_above + [far] + from_below[:0:-1])
    column = column.reshape((2 * z_count,) + own.shape)
    late = column[2 * near : 2 * (z_count - near + 1)]
    return column, theirs_early, lax.ppermute(late, "dm", partner), carried


def shards(voltages, responses, chirp_len):
    chans_local, beams, _, length = voltages.shape
    trials, chans = responses.shape[0], responses.shape[1]
    count = chans // chans_local
    z_count = count // 4
    forward, backward = (jnp.asarray(table) for table in constant_tables(length, RATE))
    local = jnp.dot(
        voltages.reshape(-1, 2 * length), forward, preferred_element_type=jnp.float32
    ).astype(jnp.bfloat16)
    local = local.reshape(chans_local, beams, 2 * length).transpose(1, 0, 2)
    resp = responses.reshape(trials, chans, 2 * length)
    mine, theirs_early, theirs_late, resp = gather_spectra(local, count, resp)
    x_me, z_me, c_me = coords(lax.axis_index("dm"), z_count)
    block = jnp.arange(count // 2, dtype=jnp.int32)
    table = ((block % z_count - z_me) % z_count) * 2 + ((block // z_count) ^ x_me)
    swap = jnp.reshape(c_me, (1,)).astype(jnp.int32)
    near = z_count // 4 + 1
    z_rel, x_rel = table // 2, table % 2
    is_late = (z_rel >= near) & (z_rel <= z_count - near)
    early_index = jnp.where(z_rel < near, z_rel, z_rel - (z_count - 2 * near + 1))
    tables = (
        table,
        jnp.where(is_late, 0, early_index * 2 + x_rel),
        jnp.where(is_late, (z_rel - near) * 2 + x_rel, 0),
        is_late.astype(jnp.int32),
    )
    detected = detect(tables, swap, mine, theirs_early, theirs_late, resp, chirp_len, backward)
    moved = lax.all_to_all(detected.transpose(1, 0, 2, 3), "beam", split_axis=1, concat_axis=2, tiled=True)
    return moved.reshape(trials, 1, -1)


def solution(mesh):
    placed = (P(("beam", "dm"), None, None, None), P("dm", "beam", None, None), P("dm"))
    return jax.shard_map(
        shards, mesh=mesh, in_specs=placed, out_specs=P("dm", "beam", None), check_vma=False
    )
```

```python
import functools
import math

import jax
import ml_dtypes
import numpy as np
import jax.numpy as jnp
from jax import lax
from jax.experimental import pallas as pl
from jax.experimental.pallas import tpu as pltpu
from jax.sharding import PartitionSpec as P

RATE = 4
CHAN_BLOCK = 256
GROUP = 8


def dft_tables(length):
    sample = jnp.arange(length, dtype=jnp.int32)
    phases = sample[:, None] * sample[None, :] % length
    angles = phases.astype(jnp.float32) * (2.0 * math.pi / length)
    cosine = jnp.cos(angles) / math.sqrt(length)
    sine_part = jnp.sin(angles) / math.sqrt(length)
    forward = jnp.concatenate(
        [jnp.concatenate([cosine, -sine_part], 1), jnp.concatenate([sine_part, cosine], 1)], 0
    )
    backward = jnp.concatenate(
        [jnp.concatenate([cosine, sine_part], 1), jnp.concatenate([-sine_part, cosine], 1)], 0
    )
    return (forward.astype(jnp.bfloat16), backward.astype(jnp.bfloat16))


def constant_tables(length, rate):
    sample = np.arange(length, dtype=np.int32)
    phases = sample[:, None] * sample[None, :] % length
    angles = phases.astype(np.float32) * np.float32(2.0 * math.pi / length)
    cosine = np.cos(angles) / np.float32(math.sqrt(length))
    sine_part = np.sin(angles) / np.float32(math.sqrt(length))
    forward = np.concatenate(
        [np.concatenate([cosine, -sine_part], 1), np.concatenate([sine_part, cosine], 1)], 0
    )
    backward = np.concatenate(
        [np.concatenate([cosine, sine_part], 1), np.concatenate([-sine_part, cosine], 1)], 0
    )
    pos = np.arange(length)
    order = rate * (pos % (length // rate)) + pos // (length // rate)
    backward = np.concatenate([backward[:, order], backward[:, length + order]], 1)
    return forward.astype(ml_dtypes.bfloat16), backward.astype(ml_dtypes.bfloat16)


def sample_order(length, rate):
    pos = jnp.arange(length, dtype=jnp.int32)
    bins = length // rate
    return rate * (pos % bins) + pos // bins


def detect_kernel(chirp_ref, table_ref, early_ref, late_ref, flag_ref, swap_ref, *refs):
    spec_refs = refs[: 3 * GROUP]
    resp_ref, back_ref, out_ref, pair_ref = refs[3 * GROUP :]
    _, beams, chans_local, width = spec_refs[0].shape
    trials = resp_ref.shape[0]
    length = width // 2
    bins = length // RATE
    chans = 2 * GROUP * chans_local
    keep = swap_ref[0] == 0
    pieces = []
    for g in range(GROUP):
        mine = spec_refs[3 * g][0]
        late = flag_ref[GROUP * pl.program_id(0) + g] != 0
        theirs = jnp.where(late, spec_refs[3 * g + 2][0], spec_refs[3 * g + 1][0])
        pieces += [jnp.where(keep, mine, theirs), jnp.where(keep, theirs, mine)]
    x = jnp.concatenate(pieces, axis=1)
    xr = x[:, :, :length].astype(jnp.float32)
    xi = x[:, :, length:].astype(jnp.float32)
    back = back_ref[...]
    pos = lax.broadcasted_iota(jnp.int32, (1, length), 1)
    t = RATE * (pos % bins) + pos // bins
    lane = lax.broadcasted_iota(jnp.int32, (1, 2 * bins), 1)
    rows = beams * chans // 2
    for d in range(trials):
        h = resp_ref[d]
        hr = h[:, :length].astype(jnp.float32)[None]
        hi = h[:, length:].astype(jnp.float32)[None]
        fr = hr * xr - hi * xi
        fi = hr * xi + hi * xr
        joined = jnp.concatenate([fr, fi], -1).reshape(beams * chans, width).astype(jnp.bfloat16)
        series = jnp.dot(joined, back, preferred_element_type=jnp.float32)
        powers = series[:, :length] ** 2 + series[:, length:] ** 2
        powers = jnp.where(t >= chirp_ref[d], powers, jnp.float32(0.0))
        half = powers[:, : length // 2] + powers[:, length // 2 :]
        pair_ref[...] = half + pltpu.roll(half, bins, 1)
        even = pair_ref[pl.ds(0, rows, stride=2), :]
        odd = pair_ref[pl.ds(1, rows, stride=2), :]
        both = jnp.where(lane < bins, even, odd) / RATE
        out_ref[:, d] = both.reshape(beams, chans // 2, 2 * bins).astype(out_ref.dtype)


def detect(tables, swap, mine, theirs_early, theirs_late, responses, chirp_len, backward):
    blocks, beams, chans_local, width = mine.shape
    trials, chans = responses.shape[0], responses.shape[1]
    length = width // 2
    bins = length // RATE
    step = 2 * GROUP * chans_local
    flops = 2 * trials * beams * chans * width * width
    bytes_accessed = 2 * (2 * mine.size + responses.size + backward.size + trials * beams * chans * bins)
    spec_specs = []
    for g in range(GROUP):
        for which in range(3):
            spec_specs.append(
                pl.BlockSpec(
                    (1, beams, chans_local, width),
                    lambda n, cl, tb, te, tl, fl, sw, g=g, which=which: (
                        (tb, te, tl)[which][GROUP * n + g], 0, 0, 0
                    ),
                )
            )
    return pl.pallas_call(
        detect_kernel,
        out_shape=jax.ShapeDtypeStruct((beams, trials, chans // 2, 2 * bins), jnp.bfloat16),
        grid_spec=pltpu.PrefetchScalarGridSpec(
            num_scalar_prefetch=6,
            grid=(chans // step,),
            in_specs=spec_specs + [
                pl.BlockSpec((trials, step, width), lambda n, cl, tb, te, tl, fl, sw: (0, n, 0)),
                pl.BlockSpec((width, width), lambda n, cl, tb, te, tl, fl, sw: (0, 0)),
            ],
            out_specs=pl.BlockSpec(
                (beams, trials, step // 2, 2 * bins), lambda n, cl, tb, te, tl, fl, sw: (0, 0, n, 0)
            ),
            scratch_shapes=[pltpu.VMEM((beams * step, 2 * bins), jnp.float32)],
        ),
        compiler_params=pltpu.CompilerParams(
            dimension_semantics=("arbitrary",), vmem_limit_bytes=48 * 1024 * 1024
        ),
        cost_estimate=pl.CostEstimate(flops=flops, transcendentals=0, bytes_accessed=bytes_accessed),
    )(chirp_len, *tables, swap, *([mine, theirs_early, theirs_late] * GROUP), responses, backward)


def coords(index, z_count):
    return index // (2 * z_count), (index // 2) % z_count, index % 2


def flat(x_lo, z, core, z_count):
    return (x_lo * z_count + z % z_count) * 2 + core


def moves(count, step):
    z_count = count // 4
    pairs = []
    for index in range(count):
        x_lo, z, core = coords(index, z_count)
        pairs.append((index, step(x_lo, z, core, z_count)))
    return pairs


def gather_spectra(own, count, carried):
    z_count = count // 4
    across = moves(count, lambda x, z, c, n: flat(1 - x, z, c, n))
    up = moves(count, lambda x, z, c, n: flat(x, z + 1, c, n))
    down = moves(count, lambda x, z, c, n: flat(x, z - 1, c, n))
    partner = moves(count, lambda x, z, c, n: flat(x, z, 1 - c, n))
    pair = jnp.stack([own, lax.ppermute(own, "dm", across)])
    from_below = [pair]
    from_above = [pair]
    for k in range(z_count // 2 - 1):
        from_below.append(lax.ppermute(from_below[-1], "dm", up))
        from_above.append(lax.ppermute(from_above[-1], "dm", down))
        if k == 0:
            from_below[-1], from_above[-1], carried = lax.optimization_barrier(
                (from_below[-1], from_above[-1], carried)
            )
    far = jnp.stack(
        [lax.ppermute(from_below[-1][0], "dm", up), lax.ppermute(from_above[-1][1], "dm", down)]
    )
    near = z_count // 4 + 1
    early = jnp.stack(from_above[:near] + from_below[near - 1 : 0 : -1])
    early = early.reshape((-1,) + own.shape)
    theirs_early = lax.ppermute(early, "dm", partner)
    column = jnp.stack(from_above + [far] + from_below[:0:-1])
    column = column.reshape((2 * z_count,) + own.shape)
    late = column[2 * near : 2 * (z_count - near + 1)]
    return column, theirs_early, lax.ppermute(late, "dm", partner), carried


def shards(voltages, responses, chirp_len):
    chans_local, beams, _, length = voltages.shape
    trials, chans = responses.shape[0], responses.shape[1]
    count = chans // chans_local
    z_count = count // 4
    forward, backward = (jnp.asarray(table) for table in constant_tables(length, RATE))
    local = jnp.dot(
        voltages.reshape(-1, 2 * length), forward, preferred_element_type=jnp.float32
    ).astype(jnp.bfloat16)
    local = local.reshape(chans_local, beams, 2 * length).transpose(1, 0, 2)
    resp = responses.reshape(trials, chans, 2 * length)
    mine, theirs_early, theirs_late, resp = gather_spectra(local, count, resp)
    x_me, z_me, c_me = coords(lax.axis_index("dm"), z_count)
    block = jnp.arange(count // 2, dtype=jnp.int32)
    table = ((block % z_count - z_me) % z_count) * 2 + ((block // z_count) ^ x_me)
    swap = jnp.reshape(c_me, (1,)).astype(jnp.int32)
    near = z_count // 4 + 1
    z_rel, x_rel = table // 2, table % 2
    is_late = (z_rel >= near) & (z_rel <= z_count - near)
    early_index = jnp.where(z_rel < near, z_rel, z_rel - (z_count - 2 * near + 1))
    tables = (
        table,
        jnp.where(is_late, 0, early_index * 2 + x_rel),
        jnp.where(is_late, (z_rel - near) * 2 + x_rel, 0),
        is_late.astype(jnp.int32),
    )
    detected = detect(tables, swap, mine, theirs_early, theirs_late, resp, chirp_len, backward)
    moved = lax.all_to_all(detected.transpose(1, 0, 2, 3), "beam", split_axis=1, concat_axis=2, tiled=True)
    return moved.reshape(trials, 1, -1)


def solution(mesh):
    placed = (P(("beam", "dm"), None, None, None), P("dm", "beam", None, None), P("dm"))
    return jax.shard_map(
        shards, mesh=mesh, in_specs=placed, out_specs=P("dm", "beam", None), check_vma=False
    )
```

```python
import functools
import math

import jax
import ml_dtypes
import numpy as np
import jax.numpy as jnp
from jax import lax
from jax.experimental import pallas as pl
from jax.experimental.pallas import tpu as pltpu
from jax.sharding import PartitionSpec as P

RATE = 4
CHAN_BLOCK = 256
GROUP = 4


def dft_tables(length):
    sample = jnp.arange(length, dtype=jnp.int32)
    phases = sample[:, None] * sample[None, :] % length
    angles = phases.astype(jnp.float32) * (2.0 * math.pi / length)
    cosine = jnp.cos(angles) / math.sqrt(length)
    sine_part = jnp.sin(angles) / math.sqrt(length)
    forward = jnp.concatenate(
        [jnp.concatenate([cosine, -sine_part], 1), jnp.concatenate([sine_part, cosine], 1)], 0
    )
    backward = jnp.concatenate(
        [jnp.concatenate([cosine, sine_part], 1), jnp.concatenate([-sine_part, cosine], 1)], 0
    )
    return (forward.astype(jnp.bfloat16), backward.astype(jnp.bfloat16))


def constant_tables(length, rate):
    sample = np.arange(length, dtype=np.int32)
    phases = sample[:, None] * sample[None, :] % length
    angles = phases.astype(np.float32) * np.float32(2.0 * math.pi / length)
    cosine = np.cos(angles) / np.float32(math.sqrt(length))
    sine_part = np.sin(angles) / np.float32(math.sqrt(length))
    forward = np.concatenate(
        [np.concatenate([cosine, -sine_part], 1), np.concatenate([sine_part, cosine], 1)], 0
    )
    backward = np.concatenate(
        [np.concatenate([cosine, sine_part], 1), np.concatenate([-sine_part, cosine], 1)], 0
    )
    pos = np.arange(length)
    order = rate * (pos % (length // rate)) + pos // (length // rate)
    backward = np.concatenate([backward[:, order], backward[:, length + order]], 1)
    return forward.astype(ml_dtypes.bfloat16), backward.astype(ml_dtypes.bfloat16)


def sample_order(length, rate):
    pos = jnp.arange(length, dtype=jnp.int32)
    bins = length // rate
    return rate * (pos % bins) + pos // bins


def detect_kernel(chirp_ref, table_ref, early_ref, late_ref, flag_ref, swap_ref, *refs):
    spec_refs = refs[: 3 * GROUP]
    resp_ref, back_ref, out_ref, pair_ref = refs[3 * GROUP :]
    _, beams, chans_local, width = spec_refs[0].shape
    trials = resp_ref.shape[0]
    length = width // 2
    bins = length // RATE
    chans = 2 * GROUP * chans_local
    keep = swap_ref[0] == 0
    pieces = []
    for g in range(GROUP):
        mine = spec_refs[3 * g][0]
        late = flag_ref[GROUP * pl.program_id(0) + g] != 0
        theirs = jnp.where(late, spec_refs[3 * g + 2][0], spec_refs[3 * g + 1][0])
        pieces += [jnp.where(keep, mine, theirs), jnp.where(keep, theirs, mine)]
    x = jnp.concatenate(pieces, axis=1)
    xr = x[:, :, :length].astype(jnp.float32)
    xi = x[:, :, length:].astype(jnp.float32)
    back = back_ref[...]
    pos = lax.broadcasted_iota(jnp.int32, (1, length), 1)
    t = RATE * (pos % bins) + pos // bins
    lane = lax.broadcasted_iota(jnp.int32, (1, 2 * bins), 1)
    rows = beams * chans // 2
    for d in range(trials):
        h = resp_ref[d]
        hr = h[:, :length].astype(jnp.float32)[None]
        hi = h[:, length:].astype(jnp.float32)[None]
        fr = hr * xr - hi * xi
        fi = hr * xi + hi * xr
        joined = jnp.concatenate([fr, fi], -1).reshape(beams * chans, width).astype(jnp.bfloat16)
        series = jnp.dot(joined, back, preferred_element_type=jnp.float32)
        powers = series[:, :length] ** 2 + series[:, length:] ** 2
        powers = jnp.where(t >= chirp_ref[d], powers, jnp.float32(0.0))
        half = powers[:, : length // 2] + powers[:, length // 2 :]
        pair_ref[...] = half + pltpu.roll(half, bins, 1)
        even = pair_ref[pl.ds(0, rows, stride=2), :]
        odd = pair_ref[pl.ds(1, rows, stride=2), :]
        both = jnp.where(lane < bins, even, odd) / RATE
        out_ref[:, :, d] = both.reshape(beams, chans // 2, 2 * bins).astype(out_ref.dtype)


def detect(tables, swap, mine, theirs_early, theirs_late, responses, chirp_len, backward):
    blocks, beams, chans_local, width = mine.shape
    trials, chans = responses.shape[0], responses.shape[1]
    length = width // 2
    bins = length // RATE
    step = 2 * GROUP * chans_local
    flops = 2 * trials * beams * chans * width * width
    bytes_accessed = 2 * (2 * mine.size + responses.size + backward.size + trials * beams * chans * bins)
    spec_specs = []
    for g in range(GROUP):
        for which in range(3):
            spec_specs.append(
                pl.BlockSpec(
                    (1, beams, chans_local, width),
                    lambda n, cl, tb, te, tl, fl, sw, g=g, which=which: (
                        (tb, te, tl)[which][GROUP * n + g], 0, 0, 0
                    ),
                )
            )
    return pl.pallas_call(
        detect_kernel,
        out_shape=jax.ShapeDtypeStruct((beams, chans // 2, trials, 2 * bins), jnp.bfloat16),
        grid_spec=pltpu.PrefetchScalarGridSpec(
            num_scalar_prefetch=6,
            grid=(chans // step,),
            in_specs=spec_specs + [
                pl.BlockSpec((trials, step, width), lambda n, cl, tb, te, tl, fl, sw: (0, n, 0)),
                pl.BlockSpec((width, width), lambda n, cl, tb, te, tl, fl, sw: (0, 0)),
            ],
            out_specs=pl.BlockSpec(
                (beams, step // 2, trials, 2 * bins), lambda n, cl, tb, te, tl, fl, sw: (0, n, 0, 0)
            ),
            scratch_shapes=[pltpu.VMEM((beams * step, 2 * bins), jnp.float32)],
        ),
        compiler_params=pltpu.CompilerParams(
            dimension_semantics=("arbitrary",), vmem_limit_bytes=48 * 1024 * 1024
        ),
        cost_estimate=pl.CostEstimate(flops=flops, transcendentals=0, bytes_accessed=bytes_accessed),
    )(chirp_len, *tables, swap, *([mine, theirs_early, theirs_late] * GROUP), responses, backward)


def coords(index, z_count):
    return index // (2 * z_count), (index // 2) % z_count, index % 2


def flat(x_lo, z, core, z_count):
    return (x_lo * z_count + z % z_count) * 2 + core


def moves(count, step):
    z_count = count // 4
    pairs = []
    for index in range(count):
        x_lo, z, core = coords(index, z_count)
        pairs.append((index, step(x_lo, z, core, z_count)))
    return pairs


def gather_spectra(own, count, carried):
    z_count = count // 4
    across = moves(count, lambda x, z, c, n: flat(1 - x, z, c, n))
    up = moves(count, lambda x, z, c, n: flat(x, z + 1, c, n))
    down = moves(count, lambda x, z, c, n: flat(x, z - 1, c, n))
    partner = moves(count, lambda x, z, c, n: flat(x, z, 1 - c, n))
    pair = jnp.stack([own, lax.ppermute(own, "dm", across)])
    from_below = [pair]
    from_above = [pair]
    for k in range(z_count // 2 - 1):
        from_below.append(lax.ppermute(from_below[-1], "dm", up))
        from_above.append(lax.ppermute(from_above[-1], "dm", down))
        if k == 0:
            from_below[-1], from_above[-1], carried = lax.optimization_barrier(
                (from_below[-1], from_above[-1], carried)
            )
    far = jnp.stack(
        [lax.ppermute(from_below[-1][0], "dm", up), lax.ppermute(from_above[-1][1], "dm", down)]
    )
    near = z_count // 4 + 1
    early = jnp.stack(from_above[:near] + from_below[near - 1 : 0 : -1])
    early = early.reshape((-1,) + own.shape)
    theirs_early = lax.ppermute(early, "dm", partner)
    column = jnp.stack(from_above + [far] + from_below[:0:-1])
    column = column.reshape((2 * z_count,) + own.shape)
    late = column[2 * near : 2 * (z_count - near + 1)]
    return column, theirs_early, lax.ppermute(late, "dm", partner), carried


def shards(voltages, responses, chirp_len):
    chans_local, beams, _, length = voltages.shape
    trials, chans = responses.shape[0], responses.shape[1]
    count = chans // chans_local
    z_count = count // 4
    forward, backward = (jnp.asarray(table) for table in constant_tables(length, RATE))
    local = jnp.dot(
        voltages.reshape(-1, 2 * length), forward, preferred_element_type=jnp.float32
    ).astype(jnp.bfloat16)
    local = local.reshape(chans_local, beams, 2 * length).transpose(1, 0, 2)
    resp = responses.reshape(trials, chans, 2 * length)
    mine, theirs_early, theirs_late, resp = gather_spectra(local, count, resp)
    x_me, z_me, c_me = coords(lax.axis_index("dm"), z_count)
    block = jnp.arange(count // 2, dtype=jnp.int32)
    table = ((block % z_count - z_me) % z_count) * 2 + ((block // z_count) ^ x_me)
    swap = jnp.reshape(c_me, (1,)).astype(jnp.int32)
    near = z_count // 4 + 1
    z_rel, x_rel = table // 2, table % 2
    is_late = (z_rel >= near) & (z_rel <= z_count - near)
    early_index = jnp.where(z_rel < near, z_rel, z_rel - (z_count - 2 * near + 1))
    tables = (
        table,
        jnp.where(is_late, 0, early_index * 2 + x_rel),
        jnp.where(is_late, (z_rel - near) * 2 + x_rel, 0),
        is_late.astype(jnp.int32),
    )
    detected = detect(tables, swap, mine, theirs_early, theirs_late, resp, chirp_len, backward)
    moved = lax.all_to_all(detected, "beam", split_axis=0, concat_axis=1, tiled=True)
    return moved[0].transpose(1, 0, 2).reshape(trials, 1, -1)


def solution(mesh):
    placed = (P(("beam", "dm"), None, None, None), P("dm", "beam", None, None), P("dm"))
    return jax.shard_map(
        shards, mesh=mesh, in_specs=placed, out_specs=P("dm", "beam", None), check_vma=False
    )
```

```python
import functools
import math

import jax
import ml_dtypes
import numpy as np
import jax.numpy as jnp
from jax import lax
from jax.experimental import pallas as pl
from jax.experimental.pallas import tpu as pltpu
from jax.sharding import PartitionSpec as P

RATE = 4
CHAN_BLOCK = 256
GROUP = 4


def dft_tables(length):
    sample = jnp.arange(length, dtype=jnp.int32)
    phases = sample[:, None] * sample[None, :] % length
    angles = phases.astype(jnp.float32) * (2.0 * math.pi / length)
    cosine = jnp.cos(angles) / math.sqrt(length)
    sine_part = jnp.sin(angles) / math.sqrt(length)
    forward = jnp.concatenate(
        [jnp.concatenate([cosine, -sine_part], 1), jnp.concatenate([sine_part, cosine], 1)], 0
    )
    backward = jnp.concatenate(
        [jnp.concatenate([cosine, sine_part], 1), jnp.concatenate([-sine_part, cosine], 1)], 0
    )
    return (forward.astype(jnp.bfloat16), backward.astype(jnp.bfloat16))


def constant_tables(length, rate):
    sample = np.arange(length, dtype=np.int32)
    phases = sample[:, None] * sample[None, :] % length
    angles = phases.astype(np.float32) * np.float32(2.0 * math.pi / length)
    cosine = np.cos(angles) / np.float32(math.sqrt(length))
    sine_part = np.sin(angles) / np.float32(math.sqrt(length))
    forward = np.concatenate(
        [np.concatenate([cosine, -sine_part], 1), np.concatenate([sine_part, cosine], 1)], 0
    )
    backward = np.concatenate(
        [np.concatenate([cosine, sine_part], 1), np.concatenate([-sine_part, cosine], 1)], 0
    )
    pos = np.arange(length)
    order = rate * (pos % (length // rate)) + pos // (length // rate)
    backward = np.concatenate([backward[:, order], backward[:, length + order]], 1)
    return forward.astype(ml_dtypes.bfloat16), backward.astype(ml_dtypes.bfloat16)


def sample_order(length, rate):
    pos = jnp.arange(length, dtype=jnp.int32)
    bins = length // rate
    return rate * (pos % bins) + pos // bins


def detect_kernel(chirp_ref, table_ref, early_ref, late_ref, flag_ref, swap_ref, *refs):
    spec_refs = refs[: 3 * GROUP]
    resp_ref, back_ref, out_ref, pair_ref = refs[3 * GROUP :]
    _, beams, chans_local, width = spec_refs[0].shape
    trials = resp_ref.shape[0]
    length = width // 2
    bins = length // RATE
    chans = 2 * GROUP * chans_local
    keep = swap_ref[0] == 0
    pieces = []
    for g in range(GROUP):
        mine = spec_refs[3 * g][0]
        late = flag_ref[GROUP * pl.program_id(0) + g] != 0
        theirs = jnp.where(late, spec_refs[3 * g + 2][0], spec_refs[3 * g + 1][0])
        pieces += [jnp.where(keep, mine, theirs), jnp.where(keep, theirs, mine)]
    x = jnp.concatenate(pieces, axis=1)
    xr = x[:, :, :length].astype(jnp.float32)
    xi = x[:, :, length:].astype(jnp.float32)
    back = back_ref[...]
    pos = lax.broadcasted_iota(jnp.int32, (1, length), 1)
    t = RATE * (pos % bins) + pos // bins
    lane = lax.broadcasted_iota(jnp.int32, (1, 2 * bins), 1)
    rows = beams * chans // 2
    for d in range(trials):
        h = resp_ref[d]
        hr = h[:, :length].astype(jnp.float32)[None]
        hi = h[:, length:].astype(jnp.float32)[None]
        fr = hr * xr - hi * xi
        fi = hr * xi + hi * xr
        joined = jnp.concatenate([fr, fi], -1).reshape(beams * chans, width).astype(jnp.bfloat16)
        series = jnp.dot(joined, back, preferred_element_type=jnp.float32)
        powers = series[:, :length] ** 2 + series[:, length:] ** 2
        powers = jnp.where(t >= chirp_ref[d], powers, jnp.float32(0.0))
        half = powers[:, : length // 2] + powers[:, length // 2 :]
        pair_ref[...] = half + pltpu.roll(half, bins, 1)
        even = pair_ref[pl.ds(0, rows, stride=2), :]
        odd = pair_ref[pl.ds(1, rows, stride=2), :]
        both = jnp.where(lane < bins, even, odd) / RATE
        out_ref[:, d] = both.reshape(beams, chans // 2, 2 * bins).astype(out_ref.dtype)


def detect(tables, swap, mine, theirs_early, theirs_late, responses, chirp_len, backward):
    blocks, beams, chans_local, width = mine.shape
    trials, chans = responses.shape[0], responses.shape[1]
    length = width // 2
    bins = length // RATE
    step = 2 * GROUP * chans_local
    flops = 2 * trials * beams * chans * width * width
    bytes_accessed = 2 * (2 * mine.size + responses.size + backward.size + trials * beams * chans * bins)
    spec_specs = []
    for g in range(GROUP):
        for which in range(3):
            spec_specs.append(
                pl.BlockSpec(
                    (1, beams, chans_local, width),
                    lambda n, cl, tb, te, tl, fl, sw, g=g, which=which: (
                        (tb, te, tl)[which][GROUP * n + g], 0, 0, 0
                    ),
                )
            )
    return pl.pallas_call(
        detect_kernel,
        out_shape=jax.ShapeDtypeStruct((beams, trials, chans // 2, 2 * bins), jnp.bfloat16),
        grid_spec=pltpu.PrefetchScalarGridSpec(
            num_scalar_prefetch=6,
            grid=(chans // step,),
            in_specs=spec_specs + [
                pl.BlockSpec((trials, step, width), lambda n, cl, tb, te, tl, fl, sw: (0, n, 0)),
                pl.BlockSpec((width, width), lambda n, cl, tb, te, tl, fl, sw: (0, 0)),
            ],
            out_specs=pl.BlockSpec(
                (beams, trials, step // 2, 2 * bins), lambda n, cl, tb, te, tl, fl, sw: (0, 0, n, 0)
            ),
            scratch_shapes=[pltpu.VMEM((beams * step, 2 * bins), jnp.float32)],
        ),
        compiler_params=pltpu.CompilerParams(
            dimension_semantics=("arbitrary",), vmem_limit_bytes=48 * 1024 * 1024
        ),
        cost_estimate=pl.CostEstimate(flops=flops, transcendentals=0, bytes_accessed=bytes_accessed),
    )(chirp_len, *tables, swap, *([mine, theirs_early, theirs_late] * GROUP), responses, backward)


def split_kernel(chirp_ref, index_ref, block_ref, swap_ref, mine_ref, theirs_ref, resp_ref, back_ref, *rest):
    out_ref, pair_ref = rest[-2], rest[-1]
    _, beams, chans_local, width = mine_ref.shape
    trials = resp_ref.shape[0]
    length = width // 2
    bins = length // RATE
    chans = 2 * chans_local
    keep = swap_ref[0] == 0
    mine = mine_ref[0]
    theirs = theirs_ref[0]
    x = jnp.concatenate([jnp.where(keep, mine, theirs), jnp.where(keep, theirs, mine)], axis=1)
    xr = x[:, :, :length].astype(jnp.float32)
    xi = x[:, :, length:].astype(jnp.float32)
    back = back_ref[...]
    pos = lax.broadcasted_iota(jnp.int32, (1, length), 1)
    t = RATE * (pos % bins) + pos // bins
    lane = lax.broadcasted_iota(jnp.int32, (1, 2 * bins), 1)
    rows = beams * chans // 2
    for d in range(trials):
        h = resp_ref[d]
        hr = h[:, :length].astype(jnp.float32)[None]
        hi = h[:, length:].astype(jnp.float32)[None]
        fr = hr * xr - hi * xi
        fi = hr * xi + hi * xr
        joined = jnp.concatenate([fr, fi], -1).reshape(beams * chans, width).astype(jnp.bfloat16)
        series = jnp.dot(joined, back, preferred_element_type=jnp.float32)
        powers = series[:, :length] ** 2 + series[:, length:] ** 2
        powers = jnp.where(t >= chirp_ref[d], powers, jnp.float32(0.0))
        half = powers[:, : length // 2] + powers[:, length // 2 :]
        pair_ref[...] = half + pltpu.roll(half, bins, 1)
        even = pair_ref[pl.ds(0, rows, stride=2), :]
        odd = pair_ref[pl.ds(1, rows, stride=2), :]
        both = jnp.where(lane < bins, even, odd) / RATE
        out_ref[:, d] = both.reshape(beams, chans // 2, 2 * bins).astype(out_ref.dtype)


def detect_part(index, block, swap, mine, theirs, responses, chirp_len, backward, previous):
    _, beams, chans_local, width = mine.shape
    trials, chans = responses.shape[0], responses.shape[1]
    bins = width // 2 // RATE
    step = 2 * chans_local
    count = index.shape[0]
    flops = 2 * trials * beams * count * step * width * width
    bytes_accessed = 2 * count * (2 * beams * chans_local * width + trials * step * width + trials * beams * step * bins)
    spec = pl.BlockSpec((1, beams, chans_local, width), lambda n, cl, ix, bk, sw: (ix[n], 0, 0, 0))
    in_specs = [
        spec,
        spec,
        pl.BlockSpec((trials, step, width), lambda n, cl, ix, bk, sw: (0, bk[n], 0)),
        pl.BlockSpec((width, width), lambda n, cl, ix, bk, sw: (0, 0)),
    ]
    args = [chirp_len, index, block, swap, mine, theirs, responses, backward]
    aliases = {}
    if previous is not None:
        in_specs.append(pl.BlockSpec(memory_space=pl.ANY))
        args.append(previous)
        aliases = {len(args) - 1: 0}
    return pl.pallas_call(
        split_kernel,
        out_shape=jax.ShapeDtypeStruct((beams, trials, chans // 2, 2 * bins), jnp.bfloat16),
        grid_spec=pltpu.PrefetchScalarGridSpec(
            num_scalar_prefetch=4,
            grid=(count,),
            in_specs=in_specs,
            out_specs=pl.BlockSpec(
                (beams, trials, step // 2, 2 * bins), lambda n, cl, ix, bk, sw: (0, 0, bk[n], 0)
            ),
            scratch_shapes=[pltpu.VMEM((beams * step, 2 * bins), jnp.float32)],
        ),
        input_output_aliases=aliases,
        compiler_params=pltpu.CompilerParams(
            dimension_semantics=("arbitrary",), vmem_limit_bytes=48 * 1024 * 1024
        ),
        cost_estimate=pl.CostEstimate(flops=flops, transcendentals=0, bytes_accessed=bytes_accessed),
    )(*args)


def coords(index, z_count):
    return index // (2 * z_count), (index // 2) % z_count, index % 2


def flat(x_lo, z, core, z_count):
    return (x_lo * z_count + z % z_count) * 2 + core


def moves(count, step):
    z_count = count // 4
    pairs = []
    for index in range(count):
        x_lo, z, core = coords(index, z_count)
        pairs.append((index, step(x_lo, z, core, z_count)))
    return pairs


def gather_spectra(own, count, carried):
    z_count = count // 4
    across = moves(count, lambda x, z, c, n: flat(1 - x, z, c, n))
    up = moves(count, lambda x, z, c, n: flat(x, z + 1, c, n))
    down = moves(count, lambda x, z, c, n: flat(x, z - 1, c, n))
    partner = moves(count, lambda x, z, c, n: flat(x, z, 1 - c, n))
    pair = jnp.stack([own, lax.ppermute(own, "dm", across)])
    from_below = [pair]
    from_above = [pair]
    for k in range(z_count // 2 - 1):
        from_below.append(lax.ppermute(from_below[-1], "dm", up))
        from_above.append(lax.ppermute(from_above[-1], "dm", down))
        if k == 0:
            from_below[-1], from_above[-1], carried = lax.optimization_barrier(
                (from_below[-1], from_above[-1], carried)
            )
    far = jnp.stack(
        [lax.ppermute(from_below[-1][0], "dm", up), lax.ppermute(from_above[-1][1], "dm", down)]
    )
    near = z_count // 4 + 1
    early = jnp.stack(from_above[:near] + from_below[near - 1 : 0 : -1])
    early = early.reshape((-1,) + own.shape)
    theirs_early = lax.ppermute(early, "dm", partner)
    column = jnp.stack(from_above + [far] + from_below[:0:-1])
    column = column.reshape((2 * z_count,) + own.shape)
    late = column[2 * near : 2 * (z_count - near + 1)]
    return early, late, theirs_early, lax.ppermute(late, "dm", partner), carried


def shards(voltages, responses, chirp_len):
    chans_local, beams, _, length = voltages.shape
    trials, chans = responses.shape[0], responses.shape[1]
    count = chans // chans_local
    z_count = count // 4
    forward, backward = (jnp.asarray(table) for table in constant_tables(length, RATE))
    local = jnp.dot(
        voltages.reshape(-1, 2 * length), forward, preferred_element_type=jnp.float32
    ).astype(jnp.bfloat16)
    local = local.reshape(chans_local, beams, 2 * length).transpose(1, 0, 2)
    resp = responses.reshape(trials, chans, 2 * length)
    mine_early, mine_late, theirs_early, theirs_late, resp = gather_spectra(local, count, resp)
    x_me, z_me, c_me = coords(lax.axis_index("dm"), z_count)
    swap = jnp.reshape(c_me, (1,)).astype(jnp.int32)
    near = z_count // 4 + 1
    x_rel = jnp.arange(2, dtype=jnp.int32)[None, :]
    early_z = jnp.array(list(range(near)) + [z_count - k for k in range(near - 1, 0, -1)], jnp.int32)
    late_z = jnp.arange(near, z_count - near + 1, dtype=jnp.int32)
    early_block = (((x_rel ^ x_me) * z_count) + (z_me + early_z[:, None]) % z_count).reshape(-1)
    late_block = (((x_rel ^ x_me) * z_count) + (z_me + late_z[:, None]) % z_count).reshape(-1)
    first = detect_part(
        jnp.arange(early_block.shape[0], dtype=jnp.int32), early_block, swap,
        mine_early, theirs_early, resp, chirp_len, backward, None,
    )
    detected = detect_part(
        jnp.arange(late_block.shape[0], dtype=jnp.int32), late_block, swap,
        mine_late, theirs_late, resp, chirp_len, backward, first,
    )
    moved = lax.all_to_all(detected.transpose(1, 0, 2, 3), "beam", split_axis=1, concat_axis=2, tiled=True)
    return moved.reshape(trials, 1, -1)


def solution(mesh):
    placed = (P(("beam", "dm"), None, None, None), P("dm", "beam", None, None), P("dm"))
    return jax.shard_map(
        shards, mesh=mesh, in_specs=placed, out_specs=P("dm", "beam", None), check_vma=False
    )
```
